32 devices in a mesh: grp: 2 (over y), blk: 8 (over z, x), bin: 2 (over core).
Axes of the slice: x: 2, y: 2, z: 4, core: 2. Of those that a mesh axis runs over, the one named last changes fastest.
Arguments:
- units: bfloat16 [1024, 32768], P(('grp', 'bin'), 'blk'), parts along dimension 0, may hold values from -6 to 6
- cotangent: bfloat16 [1024, 32768], P(('grp', 'bin'), 'blk'), parts along dimension 0, may hold values from -6 to 6
- left_factor: bfloat16 [64, 512, 512], P('blk', 'bin'), may hold values from -0.25 to 0.25
- right_factor: bfloat16 [512, 64, 64], P('blk', 'bin'), may hold values from -0.75 to 0.75
- session_units: int32 [128], P(('grp', 'blk')), parts along dimension 0, may hold values from 128 to 512, as said below
Outputs:
- grad_left: bfloat16 [128, 512, 512], P(('grp', 'blk'), 'bin'), parts along dimension 0
- grad_right: bfloat16 [1024, 64, 64], P(('grp', 'blk'), 'bin'), parts along dimension 0
The draws below stay inside these ranges and needn't reach their ends.
There are 2 independent parts, one for each index of `grp`. The reference program is written for one: setup_inputs(seed, part) draws one part's arguments, and reference() takes and returns one part's arrays. A program takes and returns all parts, laid end to end along the dimension named above; an argument that names none is the same for every part. Nothing has to cross between parts.
Inputs may be any that keep to these rules, and one draw needn't show every extreme that they name: `session_units`: each count is a multiple of a quarter of 512; some session of every group has all 512 units live.
All inputs are finite; a program needn't handle non-finite values.
Results may differ from the reference program's by a relative error of at most 0.0049.
Values may be sent and summed in bfloat16 or wider, within the bound.
No kernel may reach another device: no remote copies, remote signals or barrier semaphores. Data moves between devices by JAX's collectives and lax.ppermute only.
A program may use at most 128 MiB of HBM per device.

```python
import jax
import jax.numpy as jnp

BS = 512
NB = 64
BINS = 512
UNITS = 32768


def draw_session_units(key, part):
    first_key, second_key = jax.random.split(jax.random.fold_in(key, 17))
    quarters = jax.random.randint(first_key, (NB,), 1, 5) * (BS // 4)
    full_slot = jax.random.randint(second_key, (), 0, NB)
    return jnp.where(jnp.arange(NB) == full_slot, BS, quarters).astype(jnp.int32)


def steps_of(rng, dims, cuts, low, high):
    loudness = 1.0
    for position, parts in cuts:
        draws = jax.random.uniform(jax.random.fold_in(jax.random.fold_in(rng, 6), position), (parts,), jnp.float32, low / len(cuts), high / len(cuts))
        loudness = loudness * jnp.repeat(jnp.exp(draws), dims[position] // parts).reshape((-1,) + (1,) * (len(dims) - 1 - position))
    return loudness


def noise(rng, extent, spread, most, shards=(), dtype=jnp.bfloat16):
    loudness = steps_of(rng, extent, shards, -0.22, 0.18) if shards else 1.0
    array = jax.random.normal(rng, extent, jnp.float32) * spread * loudness
    return jnp.minimum(jnp.maximum(array, -most), most).astype(dtype)


def setup_inputs(seed: int = 0, part: int = 0) -> dict:
    key_list = jax.random.split(jax.random.key(seed), 6)
    own_keys = jax.random.split(jax.random.fold_in(key_list[5], part), 6)
    return {
        "units": noise(own_keys[0], (BINS, UNITS), 1.0, 6.0, ((0, 2), (1, 8))),
        "cotangent": noise(own_keys[1], (BINS, UNITS), 1.0, 6.0, ((0, 2), (1, 8))),
        "left_factor": noise(key_list[2], (NB, BS, BS), BS ** -0.5, 0.25, ((0, 8), (1, 2))),
        "right_factor": noise(key_list[3], (BS, NB, NB), NB ** -0.5, 0.75, ((0, 8), (1, 2))),
        "session_units": draw_session_units(jax.random.fold_in(jax.random.fold_in(key_list[5], part), 71), part),
    }


def reference(units, cotangent, left_factor, right_factor, session_units):
    bin_count = units.shape[0]
    unit_mask = (jnp.arange(BS)[None, :] < session_units[:, None]).astype(jnp.bfloat16)
    inputs = units.reshape(bin_count, NB, BS) * unit_mask[None]
    mixed = jnp.einsum("rki,kij->rjk", inputs.astype(jnp.float32), left_factor.astype(jnp.float32)).astype(jnp.bfloat16)
    upstream = cotangent.reshape(bin_count, BS, NB)
    grad_right = jnp.einsum("rjk,rjm->jkm", mixed.astype(jnp.float32), upstream.astype(jnp.float32)).astype(jnp.bfloat16)
    returned = jnp.einsum("rjm,jkm->rjk", upstream.astype(jnp.float32), right_factor.astype(jnp.float32)).astype(jnp.bfloat16)
    grad_left = jnp.einsum("rki,rjk->kij", inputs.astype(jnp.float32), returned.astype(jnp.float32)).astype(jnp.bfloat16)
    return (grad_left, grad_right)
```

```python
import jax
import jax.numpy as jnp
from jax import lax
from jax.sharding import PartitionSpec as P


def on_device(units, cotangent, left_factor, right_factor, session_units):
    row_count = units.shape[0]
    local_blocks = left_factor.shape[0]
    block_size = left_factor.shape[2]
    right_local = right_factor.shape[0]
    order_right = right_factor.shape[2]
    peer_count = lax.axis_size("blk")
    block_count = peer_count * local_blocks
    half = block_count // 2
    core = lax.axis_index("bin")

    upstream = cotangent.reshape(row_count, right_local, order_right)
    right_full = lax.all_gather(right_factor, "bin", axis=1, tiled=True)
    back_grad = jnp.einsum(
        "rjm,jkm->kjr", upstream, right_full, preferred_element_type=jnp.float32
    ).astype(jnp.bfloat16)
    back_sent = back_grad.reshape(peer_count, local_blocks, right_local, row_count)
    back_got = lax.all_to_all(back_sent, "blk", 0, 0, tiled=True)

    unit_mask = (jnp.arange(block_size)[None, :] < session_units[:, None]).astype(jnp.bfloat16)
    inputs = units.reshape(row_count, local_blocks, block_size) * unit_mask[None]
    left_full = lax.all_gather(left_factor, "bin", axis=1, tiled=True)
    mixed = jnp.einsum(
        "rki,kij->jkr", inputs, left_full, preferred_element_type=jnp.float32
    ).astype(jnp.bfloat16)
    mixed_sent = mixed.reshape(peer_count, right_local, local_blocks, row_count)
    mixed_sent, back_got = lax.optimization_barrier((mixed_sent, back_got))

    back_t = back_got.transpose(1, 0, 2, 3).reshape(local_blocks, block_size, row_count)
    left_term = jnp.einsum("rki,kjr->kij", inputs, back_t, preferred_element_type=jnp.float32)
    mixed_sent, left_term = lax.optimization_barrier((mixed_sent, left_term))
    grad_left = lax.psum_scatter(left_term, "bin", scatter_dimension=1, tiled=True).astype(
        jnp.bfloat16
    )
    mixed_got = lax.all_to_all(mixed_sent, "blk", 0, 0, tiled=True)

    mixed_t = mixed_got.transpose(1, 0, 2, 3).reshape(right_local, block_count, row_count)
    right_term = jnp.einsum("jkr,rjm->jkm", mixed_t, upstream, preferred_element_type=jnp.float32)
    mine = lax.dynamic_slice_in_dim(right_term, core * half, half, axis=1)
    theirs = lax.dynamic_slice_in_dim(right_term, (1 - core) * half, half, axis=1)
    got = lax.ppermute(theirs, "bin", [(0, 1), (1, 0)])
    grad_right = (mine + got).astype(jnp.bfloat16)
    return (grad_left, grad_right)


def solution(mesh):
    placed = (
        P(("grp", "bin"), "blk"),
        P(("grp", "bin"), "blk"),
        P("blk", "bin", None),
        P("blk", "bin", None),
        P(("grp", "blk")),
    )
    return jax.shard_map(
        on_device,
        mesh=mesh,
        in_specs=placed,
        out_specs=(P(("grp", "blk"), "bin", None), P(("grp", "blk"), "bin", None)),
        check_vma=False,
    )
```

```python
import jax
import jax.numpy as jnp
from jax import lax
from jax.sharding import PartitionSpec as P


def swap_halves(local, axis):
    other = lax.ppermute(local, "bin", [(0, 1), (1, 0)])
    core = lax.axis_index("bin")
    first = jnp.where(core == 0, local, other)
    second = jnp.where(core == 0, other, local)
    return jnp.concatenate([first, second], axis=axis)


def sum_halves(term, axis):
    half = term.shape[axis] // 2
    core = lax.axis_index("bin")
    mine = lax.dynamic_slice_in_dim(term, core * half, half, axis=axis)
    theirs = lax.dynamic_slice_in_dim(term, (1 - core) * half, half, axis=axis)
    return mine + lax.ppermute(theirs, "bin", [(0, 1), (1, 0)])


def on_device(units, cotangent, left_factor, right_factor, session_units):
    row_count = units.shape[0]
    local_blocks = left_factor.shape[0]
    block_size = left_factor.shape[2]
    right_local = right_factor.shape[0]
    order_right = right_factor.shape[2]
    peer_count = lax.axis_size("blk")
    block_count = peer_count * local_blocks

    upstream = cotangent.reshape(row_count, right_local, order_right)
    right_full = swap_halves(right_factor, 1)
    back_grad = jnp.einsum(
        "rjm,jkm->kjr", upstream, right_full, preferred_element_type=jnp.float32
    ).astype(jnp.bfloat16)
    back_sent = back_grad.reshape(peer_count, local_blocks, right_local, row_count)
    back_got = lax.all_to_all(back_sent, "blk", 0, 0, tiled=True)

    unit_mask = (jnp.arange(block_size)[None, :] < session_units[:, None]).astype(jnp.bfloat16)
    inputs = units.reshape(row_count, local_blocks, block_size) * unit_mask[None]
    left_full = swap_halves(left_factor, 1)
    mixed = jnp.einsum(
        "rki,kij->jkr", inputs, left_full, preferred_element_type=jnp.float32
    ).astype(jnp.bfloat16)
    mixed_sent = mixed.reshape(peer_count, right_local, local_blocks, row_count)
    mixed_sent, back_got = lax.optimization_barrier((mixed_sent, back_got))

    back_t = back_got.transpose(1, 0, 2, 3).reshape(local_blocks, block_size, row_count)
    left_term = jnp.einsum("rki,kjr->kij", inputs, back_t, preferred_element_type=jnp.float32)
    mixed_sent, left_term = lax.optimization_barrier((mixed_sent, left_term))
    grad_left = sum_halves(left_term, 1).astype(jnp.bfloat16)
    mixed_got = lax.all_to_all(mixed_sent, "blk", 0, 0, tiled=True)

    mixed_t = mixed_got.transpose(1, 0, 2, 3).reshape(right_local, block_count, row_count)
    right_term = jnp.einsum("jkr,rjm->jkm", mixed_t, upstream, preferred_element_type=jnp.float32)
    grad_right = sum_halves(right_term, 1).astype(jnp.bfloat16)
    return (grad_left, grad_right)


def solution(mesh):
    placed = (
        P(("grp", "bin"), "blk"),
        P(("grp", "bin"), "blk"),
        P("blk", "bin", None),
        P("blk", "bin", None),
        P(("grp", "blk")),
    )
    return jax.shard_map(
        on_device,
        mesh=mesh,
        in_specs=placed,
        out_specs=(P(("grp", "blk"), "bin", None), P(("grp", "blk"), "bin", None)),
        check_vma=False,
    )
```

```python
import jax
import jax.numpy as jnp
from jax import lax
from jax.sharding import PartitionSpec as P


def swap_halves(local, axis):
    other = lax.ppermute(local, "bin", [(0, 1), (1, 0)])
    core = lax.axis_index("bin")
    first = jnp.where(core == 0, local, other)
    second = jnp.where(core == 0, other, local)
    return jnp.concatenate([first, second], axis=axis)


def sum_halves(term, axis):
    half = term.shape[axis] // 2
    core = lax.axis_index("bin")
    mine = lax.dynamic_slice_in_dim(term, core * half, half, axis=axis)
    theirs = lax.dynamic_slice_in_dim(term, (1 - core) * half, half, axis=axis)
    return mine + lax.ppermute(theirs, "bin", [(0, 1), (1, 0)])


def on_device(units, cotangent, left_factor, right_factor, session_units):
    row_count = units.shape[0]
    local_blocks = left_factor.shape[0]
    block_size = left_factor.shape[2]
    right_local = right_factor.shape[0]
    order_right = right_factor.shape[2]
    peer_count = lax.axis_size("blk")
    block_count = peer_count * local_blocks

    upstream = cotangent.reshape(row_count, right_local, order_right)
    right_full = swap_halves(right_factor, 1)
    back_grad = jnp.einsum(
        "rjm,jkm->kjr", upstream, right_full, preferred_element_type=jnp.float32
    ).astype(jnp.bfloat16)
    back_sent = back_grad.reshape(peer_count, local_blocks, right_local, row_count)
    back_got = lax.all_to_all(back_sent, "blk", 0, 0, tiled=True)

    unit_mask = (jnp.arange(block_size)[None, :] < session_units[:, None]).astype(jnp.bfloat16)
    inputs = units.reshape(row_count, local_blocks, block_size) * unit_mask[None]
    left_full = swap_halves(left_factor, 1)
    mixed = jnp.einsum(
        "rki,kij->jkr", inputs, left_full, preferred_element_type=jnp.float32
    ).astype(jnp.bfloat16)
    mixed_sent = mixed.reshape(peer_count, right_local, local_blocks, row_count).transpose(0, 2, 1, 3)
    mixed_sent, back_got = lax.optimization_barrier((mixed_sent, back_got))

    half_size = block_size // 2
    core = lax.axis_index("bin")
    back_t = back_got.transpose(1, 0, 2, 3).reshape(local_blocks, block_size, row_count)

    def left_of(start):
        rows = lax.dynamic_slice_in_dim(inputs, start, half_size, axis=2)
        return jnp.einsum("rki,kjr->kij", rows, back_t, preferred_element_type=jnp.float32)

    theirs = left_of((1 - core) * half_size)
    mixed_sent, theirs = lax.optimization_barrier((mixed_sent, theirs))
    mixed_got = lax.all_to_all(mixed_sent, "blk", 0, 0, tiled=True)
    got_left = lax.ppermute(theirs, "bin", [(0, 1), (1, 0)])
    grad_left = (left_of(core * half_size) + got_left).astype(jnp.bfloat16)

    mixed_t = mixed_got.transpose(2, 0, 1, 3).reshape(right_local, block_count, row_count)
    grad_left, mixed_t = lax.optimization_barrier((grad_left, mixed_t))
    right_term = jnp.einsum("jkr,rjm->jkm", mixed_t, upstream, preferred_element_type=jnp.float32)
    grad_right = sum_halves(right_term, 1).astype(jnp.bfloat16)
    return (grad_left, grad_right)


def solution(mesh):
    placed = (
        P(("grp", "bin"), "blk"),
        P(("grp", "bin"), "blk"),
        P("blk", "bin", None),
        P("blk", "bin", None),
        P(("grp", "blk")),
    )
    return jax.shard_map(
        on_device,
        mesh=mesh,
        in_specs=placed,
        out_specs=(P(("grp", "blk"), "bin", None), P(("grp", "blk"), "bin", None)),
        check_vma=False,
    )
```

```python
import jax
import jax.numpy as jnp
from jax import lax
from jax.sharding import PartitionSpec as P


def swap_halves(local, axis):
    other = lax.ppermute(local, "bin", [(0, 1), (1, 0)])
    core = lax.axis_index("bin")
    first = jnp.where(core == 0, local, other)
    second = jnp.where(core == 0, other, local)
    return jnp.concatenate([first, second], axis=axis)


def on_device(units, cotangent, left_factor, right_factor, session_units):
    row_count = units.shape[0]
    local_blocks = left_factor.shape[0]
    block_size = left_factor.shape[2]
    right_local = right_factor.shape[0]
    order_right = right_factor.shape[2]
    peer_count = lax.axis_size("blk")
    block_count = peer_count * local_blocks

    upstream = cotangent.reshape(row_count, right_local, order_right)
    right_full = swap_halves(right_factor, 1)
    back_grad = jnp.einsum(
        "rjm,jkm->kjr", upstream, right_full, preferred_element_type=jnp.float32
    ).astype(jnp.bfloat16)
    back_sent = back_grad.reshape(peer_count, local_blocks, right_local, row_count)
    back_got = lax.all_to_all(back_sent, "blk", 0, 0, tiled=True)

    unit_mask = (jnp.arange(block_size)[None, :] < session_units[:, None]).astype(jnp.bfloat16)
    inputs = units.reshape(row_count, local_blocks, block_size) * unit_mask[None]
    left_full = swap_halves(left_factor, 1)
    mixed = jnp.einsum(
        "rki,kij->jkr", inputs, left_full, preferred_element_type=jnp.float32
    ).astype(jnp.bfloat16)
    mixed_sent = mixed.reshape(peer_count, right_local, local_blocks, row_count).transpose(0, 2, 1, 3)
    mixed_sent, back_got = lax.optimization_barrier((mixed_sent, back_got))

    half_size = block_size // 2
    core = lax.axis_index("bin")
    back_t = back_got.transpose(1, 0, 2, 3).reshape(local_blocks, block_size, row_count)

    def left_of(start):
        rows = lax.dynamic_slice_in_dim(inputs, start, half_size, axis=2)
        return jnp.einsum("rki,kjr->kij", rows, back_t, preferred_element_type=jnp.float32)

    theirs = left_of((1 - core) * half_size)
    mixed_sent, theirs = lax.optimization_barrier((mixed_sent, theirs))
    mixed_got = lax.all_to_all(mixed_sent, "blk", 0, 0, tiled=True)
    got_left = lax.ppermute(theirs, "bin", [(0, 1), (1, 0)])
    grad_left = (lax.optimization_barrier(left_of(core * half_size)) + got_left).astype(jnp.bfloat16)
    grad_left, mixed_got = lax.optimization_barrier((grad_left, mixed_got))
    half_peers = peer_count // 2

    def right_of(start):
        blocks = lax.dynamic_slice_in_dim(mixed_got, start, half_peers, axis=0)
        blocks = blocks.transpose(2, 0, 1, 3).reshape(right_local, half_peers * local_blocks, row_count)
        return jnp.einsum("jkr,rjm->jkm", blocks, upstream, preferred_element_type=jnp.float32)

    got_right = lax.ppermute(right_of((1 - core) * half_peers), "bin", [(0, 1), (1, 0)])
    grad_right = (lax.optimization_barrier(right_of(core * half_peers)) + got_right).astype(
        jnp.bfloat16
    )
    return (grad_left, grad_right)


def solution(mesh):
    placed = (
        P(("grp", "bin"), "blk"),
        P(("grp", "bin"), "blk"),
        P("blk", "bin", None),
        P("blk", "bin", None),
        P(("grp", "blk")),
    )
    return jax.shard_map(
        on_device,
        mesh=mesh,
        in_specs=placed,
        out_specs=(P(("grp", "blk"), "bin", None), P(("grp", "blk"), "bin", None)),
        check_vma=False,
    )
```

```python
import jax
import jax.numpy as jnp
from jax import lax
from jax.sharding import PartitionSpec as P


def swap_halves(local, axis):
    other = lax.ppermute(local, "bin", [(0, 1), (1, 0)])
    core = lax.axis_index("bin")
    first = jnp.where(core == 0, local, other)
    second = jnp.where(core == 0, other, local)
    return jnp.concatenate([first, second], axis=axis)


def on_device(units, cotangent, left_factor, right_factor, session_units):
    row_count = units.shape[0]
    local_blocks = left_factor.shape[0]
    block_size = left_factor.shape[2]
    right_local = right_factor.shape[0]
    order_right = right_factor.shape[2]
    peer_count = lax.axis_size("blk")
    block_count = peer_count * local_blocks

    upstream = cotangent.reshape(row_count, right_local, order_right)
    right_full = swap_halves(right_factor, 1)
    back_grad = jnp.einsum(
        "rjm,jkm->kjr", upstream, right_full, preferred_element_type=jnp.float32
    ).astype(jnp.bfloat16)
    back_sent = back_grad.reshape(peer_count, local_blocks, right_local, row_count)
    back_got = lax.all_to_all(back_sent, "blk", 0, 0, tiled=True)

    unit_mask = (jnp.arange(block_size)[None, :] < session_units[:, None]).astype(jnp.bfloat16)
    inputs = units.reshape(row_count, local_blocks, block_size) * unit_mask[None]
    left_full = swap_halves(left_factor, 1)
    mixed = jnp.einsum(
        "rki,kij->jkr", inputs, left_full, preferred_element_type=jnp.float32
    ).astype(jnp.bfloat16)
    mixed_sent = mixed.reshape(peer_count, right_local, local_blocks, row_count).transpose(0, 2, 1, 3)
    mixed_sent, back_got = lax.optimization_barrier((mixed_sent, back_got))

    half_size = block_size // 2
    core = lax.axis_index("bin")
    back_t = back_got.transpose(1, 0, 2, 3).reshape(local_blocks, block_size, row_count)

    def left_of(start, back_part):
        rows = lax.dynamic_slice_in_dim(inputs, start, half_size, axis=2)
        return jnp.einsum("rki,kjr->kij", rows, back_part, preferred_element_type=jnp.float32)

    half_cols = block_size // 2
    theirs_start = (1 - core) * half_size
    theirs_a = left_of(theirs_start, back_t[:, :half_cols])
    mixed_sent, theirs_a = lax.optimization_barrier((mixed_sent, theirs_a))
    mixed_got = lax.all_to_all(mixed_sent, "blk", 0, 0, tiled=True)
    got_a = lax.ppermute(theirs_a, "bin", [(0, 1), (1, 0)])
    got_b = lax.ppermute(left_of(theirs_start, back_t[:, half_cols:]), "bin", [(0, 1), (1, 0)])
    got_left = jnp.concatenate([got_a, got_b], axis=2)
    mine = lax.optimization_barrier(left_of(core * half_size, back_t))
    grad_left = (mine + got_left).astype(jnp.bfloat16)
    grad_left, mixed_got = lax.optimization_barrier((grad_left, mixed_got))
    half_peers = peer_count // 2

    def right_of(start):
        blocks = lax.dynamic_slice_in_dim(mixed_got, start, half_peers, axis=0)
        blocks = blocks.transpose(2, 0, 1, 3).reshape(right_local, half_peers * local_blocks, row_count)
        return jnp.einsum("jkr,rjm->jkm", blocks, upstream, preferred_element_type=jnp.float32)

    got_right = lax.ppermute(right_of((1 - core) * half_peers), "bin", [(0, 1), (1, 0)])
    grad_right = (lax.optimization_barrier(right_of(core * half_peers)) + got_right).astype(
        jnp.bfloat16
    )
    return (grad_left, grad_right)


def solution(mesh):
    placed = (
        P(("grp", "bin"), "blk"),
        P(("grp", "bin"), "blk"),
        P("blk", "bin", None),
        P("blk", "bin", None),
        P(("grp", "blk")),
    )
    return jax.shard_map(
        on_device,
        mesh=mesh,
        in_specs=placed,
        out_specs=(P(("grp", "blk"), "bin", None), P(("grp", "blk"), "bin", None)),
        check_vma=False,
    )
```

```python
import functools

import jax
import jax.numpy as jnp
from jax import lax
from jax.sharding import PartitionSpec as P
from jax.experimental import pallas as pl
from jax.experimental.pallas import tpu as pltpu


def _back_kernel(peer_count, local_blocks, group, cot_ref, right_ref, out_ref):
    right_local, block_count, order = right_ref.shape
    row_count = cot_ref.shape[0]
    width = group * order

    def body(step, carry):
        start = pl.multiple_of(step * width, width)
        cols = cot_ref[:, pl.ds(start, width)]
        for h in range(group):
            j = step * group + h
            part = cols[:, h * order:(h + 1) * order]
            res = lax.dot_general(
                right_ref[j], part, (((1,), (1,)), ((), ())), preferred_element_type=jnp.float32
            )
            for p in range(peer_count):
                out_ref[p, j] = res[p * local_blocks:(p + 1) * local_blocks].astype(out_ref.dtype)
        return carry

    lax.fori_loop(0, right_local // group, body, 0)


def back_grads(cotangent, right_full, peer_count, local_blocks):
    right_local, block_count, order = right_full.shape
    row_count = cotangent.shape[0]
    group = max(1, 128 // order)
    return pl.pallas_call(
        functools.partial(_back_kernel, peer_count, local_blocks, group),
        out_shape=jax.ShapeDtypeStruct((peer_count, right_local, local_blocks, row_count), jnp.bfloat16),
        in_specs=[pl.BlockSpec(memory_space=pltpu.VMEM)] * 2,
        out_specs=pl.BlockSpec(memory_space=pltpu.VMEM),
        cost_estimate=pl.CostEstimate(
            flops=2 * row_count * right_local * block_count * order,
            bytes_accessed=2 * (cotangent.size + right_full.size + row_count * right_local * block_count),
            transcendentals=0,
        ),
    )(cotangent, right_full)


def swap_halves(local, axis):
    other = lax.ppermute(local, "bin", [(0, 1), (1, 0)])
    core = lax.axis_index("bin")
    first = jnp.where(core == 0, local, other)
    second = jnp.where(core == 0, other, local)
    return jnp.concatenate([first, second], axis=axis)


def on_device(units, cotangent, left_factor, right_factor, session_units):
    row_count = units.shape[0]
    local_blocks = left_factor.shape[0]
    block_size = left_factor.shape[2]
    right_local = right_factor.shape[0]
    order_right = right_factor.shape[2]
    peer_count = lax.axis_size("blk")
    block_count = peer_count * local_blocks

    upstream = cotangent.reshape(row_count, right_local, order_right)
    right_full = swap_halves(right_factor, 1)
    back_sent = back_grads(cotangent, right_full, peer_count, local_blocks).transpose(0, 2, 1, 3)
    back_got = lax.all_to_all(back_sent, "blk", 0, 0, tiled=True)

    unit_mask = (jnp.arange(block_size)[None, :] < session_units[:, None]).astype(jnp.bfloat16)
    inputs = units.reshape(row_count, local_blocks, block_size) * unit_mask[None]
    left_full = swap_halves(left_factor, 1)
    mixed = jnp.einsum(
        "rki,kij->jkr", inputs, left_full, preferred_element_type=jnp.float32
    ).astype(jnp.bfloat16)
    mixed_sent = mixed.reshape(peer_count, right_local, local_blocks, row_count).transpose(0, 2, 1, 3)
    mixed_sent, back_got = lax.optimization_barrier((mixed_sent, back_got))

    half_size = block_size // 2
    core = lax.axis_index("bin")
    back_t = back_got.transpose(1, 0, 2, 3).reshape(local_blocks, block_size, row_count)

    def left_of(start, back_part):
        rows = lax.dynamic_slice_in_dim(inputs, start, half_size, axis=2)
        return jnp.einsum("rki,kjr->kij", rows, back_part, preferred_element_type=jnp.float32)

    half_cols = block_size // 2
    theirs_start = (1 - core) * half_size
    theirs_a = left_of(theirs_start, back_t[:, :half_cols])
    mixed_sent, theirs_a = lax.optimization_barrier((mixed_sent, theirs_a))
    mixed_got = lax.all_to_all(mixed_sent, "blk", 0, 0, tiled=True)
    got_a = lax.ppermute(theirs_a, "bin", [(0, 1), (1, 0)])
    got_b = lax.ppermute(left_of(theirs_start, back_t[:, half_cols:]), "bin", [(0, 1), (1, 0)])
    got_left = jnp.concatenate([got_a, got_b], axis=2)
    mine = lax.optimization_barrier(left_of(core * half_size, back_t))
    grad_left = (mine + got_left).astype(jnp.bfloat16)
    grad_left, mixed_got = lax.optimization_barrier((grad_left, mixed_got))
    half_peers = peer_count // 2

    def right_of(start):
        blocks = lax.dynamic_slice_in_dim(mixed_got, start, half_peers, axis=0)
        blocks = blocks.transpose(2, 0, 1, 3).reshape(right_local, half_peers * local_blocks, row_count)
        return jnp.einsum("jkr,rjm->jkm", blocks, upstream, preferred_element_type=jnp.float32)

    got_right = lax.ppermute(right_of((1 - core) * half_peers), "bin", [(0, 1), (1, 0)])
    grad_right = (lax.optimization_barrier(right_of(core * half_peers)) + got_right).astype(
        jnp.bfloat16
    )
    return (grad_left, grad_right)


def solution(mesh):
    placed = (
        P(("grp", "bin"), "blk"),
        P(("grp", "bin"), "blk"),
        P("blk", "bin", None),
        P("blk", "bin", None),
        P(("grp", "blk")),
    )
    return jax.shard_map(
        on_device,
        mesh=mesh,
        in_specs=placed,
        out_specs=(P(("grp", "blk"), "bin", None), P(("grp", "blk"), "bin", None)),
        check_vma=False,
    )
```

```python
import jax
import jax.numpy as jnp
from jax import lax
from jax.sharding import PartitionSpec as P


def swap_halves(local, axis):
    other = lax.ppermute(local, "bin", [(0, 1), (1, 0)])
    core = lax.axis_index("bin")
    first = jnp.where(core == 0, local, other)
    second = jnp.where(core == 0, other, local)
    return jnp.concatenate([first, second], axis=axis)


def on_device(units, cotangent, left_factor, right_factor, session_units):
    row_count = units.shape[0]
    local_blocks = left_factor.shape[0]
    block_size = left_factor.shape[2]
    right_local = right_factor.shape[0]
    order_right = right_factor.shape[2]
    peer_count = lax.axis_size("blk")
    block_count = peer_count * local_blocks

    upstream = cotangent.reshape(row_count, right_local, order_right)
    right_full = swap_halves(right_factor, 1)
    back_grad = jnp.einsum(
        "rjm,jkm->kjr", upstream, right_full, preferred_element_type=jnp.float32
    ).astype(jnp.bfloat16)
    back_sent = back_grad.reshape(peer_count, local_blocks, right_local, row_count)
    back_got = lax.all_to_all(back_sent, "blk", 0, 0, tiled=True)

    unit_mask = (jnp.arange(block_size)[None, :] < session_units[:, None]).astype(jnp.bfloat16)
    inputs = units.reshape(row_count, local_blocks, block_size) * unit_mask[None]
    left_full = swap_halves(left_factor, 1)
    mixed = jnp.einsum(
        "rki,kij->jkr", inputs, left_full, preferred_element_type=jnp.float32
    ).astype(jnp.bfloat16)
    mixed_sent = mixed.reshape(peer_count, right_local, local_blocks, row_count).transpose(0, 2, 1, 3)
    mixed_sent, back_got = lax.optimization_barrier((mixed_sent, back_got))

    half_size = block_size // 2
    core = lax.axis_index("bin")
    swap = [(0, 1), (1, 0)]
    own_part = lax.dynamic_slice_in_dim(inputs, core * half_size, half_size, axis=2)
    their_part = lax.dynamic_slice_in_dim(inputs, (1 - core) * half_size, half_size, axis=2)
    partner_part = lax.ppermute(their_part, "bin", swap)
    back_t = back_got.transpose(1, 0, 2, 3).reshape(local_blocks, block_size, row_count)
    partner_back = lax.ppermute(back_t, "bin", swap)
    mixed_got = lax.all_to_all(mixed_sent, "blk", 0, 0, tiled=True)
    left_term = jnp.einsum("rki,kjr->kij", own_part, back_t, preferred_element_type=jnp.float32)
    left_term = left_term + jnp.einsum(
        "rki,kjr->kij", partner_part, partner_back, preferred_element_type=jnp.float32
    )
    grad_left = left_term.astype(jnp.bfloat16)
    grad_left, mixed_got = lax.optimization_barrier((grad_left, mixed_got))
    half_peers = peer_count // 2

    def right_of(start):
        blocks = lax.dynamic_slice_in_dim(mixed_got, start, half_peers, axis=0)
        blocks = blocks.transpose(2, 0, 1, 3).reshape(right_local, half_peers * local_blocks, row_count)
        return jnp.einsum("jkr,rjm->jkm", blocks, upstream, preferred_element_type=jnp.float32)

    got_right = lax.ppermute(right_of((1 - core) * half_peers), "bin", [(0, 1), (1, 0)])
    grad_right = (lax.optimization_barrier(right_of(core * half_peers)) + got_right).astype(
        jnp.bfloat16
    )
    return (grad_left, grad_right)


def solution(mesh):
    placed = (
        P(("grp", "bin"), "blk"),
        P(("grp", "bin"), "blk"),
        P("blk", "bin", None),
        P("blk", "bin", None),
        P(("grp", "blk")),
    )
    return jax.shard_map(
        on_device,
        mesh=mesh,
        in_specs=placed,
        out_specs=(P(("grp", "blk"), "bin", None), P(("grp", "blk"), "bin", None)),
        check_vma=False,
    )
```

```python
import jax
import jax.numpy as jnp
from jax import lax
from jax.sharding import PartitionSpec as P


def swap_halves(local, axis):
    other = lax.ppermute(local, "bin", [(0, 1), (1, 0)])
    core = lax.axis_index("bin")
    first = jnp.where(core == 0, local, other)
    second = jnp.where(core == 0, other, local)
    return jnp.concatenate([first, second], axis=axis)


def exchange(sent):
    peer_count = sent.shape[0]
    me = lax.axis_index("blk")
    pieces = [lax.dynamic_index_in_dim(sent, me, 0, keepdims=False)]
    for shift in range(1, peer_count):
        piece = lax.dynamic_index_in_dim(sent, (me + shift) % peer_count, 0, keepdims=False)
        pairs = [(i, (i + shift) % peer_count) for i in range(peer_count)]
        pieces.append(lax.ppermute(piece, "blk", pairs))
    return jnp.take(jnp.stack(pieces), (me - jnp.arange(peer_count)) % peer_count, axis=0)


def on_device(units, cotangent, left_factor, right_factor, session_units):
    row_count = units.shape[0]
    local_blocks = left_factor.shape[0]
    block_size = left_factor.shape[2]
    right_local = right_factor.shape[0]
    order_right = right_factor.shape[2]
    peer_count = lax.axis_size("blk")
    block_count = peer_count * local_blocks

    upstream = cotangent.reshape(row_count, right_local, order_right)
    right_full = swap_halves(right_factor, 1)
    back_grad = jnp.einsum(
        "rjm,jkm->kjr", upstream, right_full, preferred_element_type=jnp.float32
    ).astype(jnp.bfloat16)
    back_sent = back_grad.reshape(peer_count, local_blocks, right_local, row_count)
    back_got = exchange(back_sent)

    unit_mask = (jnp.arange(block_size)[None, :] < session_units[:, None]).astype(jnp.bfloat16)
    inputs = units.reshape(row_count, local_blocks, block_size) * unit_mask[None]
    left_full = swap_halves(left_factor, 1)
    mixed = jnp.einsum(
        "rki,kij->jkr", inputs, left_full, preferred_element_type=jnp.float32
    ).astype(jnp.bfloat16)
    mixed_sent = mixed.reshape(peer_count, right_local, local_blocks, row_count).transpose(0, 2, 1, 3)

    half_size = block_size // 2
    core = lax.axis_index("bin")
    swap = [(0, 1), (1, 0)]
    own_part = lax.dynamic_slice_in_dim(inputs, core * half_size, half_size, axis=2)
    their_part = lax.dynamic_slice_in_dim(inputs, (1 - core) * half_size, half_size, axis=2)
    partner_part = lax.ppermute(their_part, "bin", swap)
    back_t = back_got.transpose(1, 0, 2, 3).reshape(local_blocks, block_size, row_count)
    partner_back = lax.ppermute(back_t, "bin", swap)
    mixed_got = lax.all_to_all(mixed_sent, "blk", 0, 0, tiled=True)
    left_term = jnp.einsum("rki,kjr->kij", own_part, back_t, preferred_element_type=jnp.float32)
    left_term = left_term + jnp.einsum(
        "rki,kjr->kij", partner_part, partner_back, preferred_element_type=jnp.float32
    )
    grad_left = left_term.astype(jnp.bfloat16)
    grad_left, mixed_got = lax.optimization_barrier((grad_left, mixed_got))
    half_peers = peer_count // 2

    def right_of(start):
        blocks = lax.dynamic_slice_in_dim(mixed_got, start, half_peers, axis=0)
        blocks = blocks.transpose(2, 0, 1, 3).reshape(right_local, half_peers * local_blocks, row_count)
        return jnp.einsum("jkr,rjm->jkm", blocks, upstream, preferred_element_type=jnp.float32)

    got_right = lax.ppermute(right_of((1 - core) * half_peers), "bin", [(0, 1), (1, 0)])
    grad_right = (lax.optimization_barrier(right_of(core * half_peers)) + got_right).astype(
        jnp.bfloat16
    )
    return (grad_left, grad_right)


def solution(mesh):
    placed = (
        P(("grp", "bin"), "blk"),
        P(("grp", "bin"), "blk"),
        P("blk", "bin", None),
        P("blk", "bin", None),
        P(("grp", "blk")),
    )
    return jax.shard_map(
        on_device,
        mesh=mesh,
        in_specs=placed,
        out_specs=(P(("grp", "blk"), "bin", None), P(("grp", "blk"), "bin", None)),
        check_vma=False,
    )
```

```python
import jax
import jax.numpy as jnp
from jax import lax
from jax.sharding import PartitionSpec as P
from jax.experimental.layout import Layout, with_layout_constraint


def swap_halves(local, axis):
    other = lax.ppermute(local, "bin", [(0, 1), (1, 0)])
    core = lax.axis_index("bin")
    first = jnp.where(core == 0, local, other)
    second = jnp.where(core == 0, other, local)
    return jnp.concatenate([first, second], axis=axis)


def on_device(units, cotangent, left_factor, right_factor, session_units):
    row_count = units.shape[0]
    local_blocks = left_factor.shape[0]
    block_size = left_factor.shape[2]
    right_local = right_factor.shape[0]
    order_right = right_factor.shape[2]
    peer_count = lax.axis_size("blk")
    block_count = peer_count * local_blocks

    upstream = cotangent.reshape(row_count, right_local, order_right)
    right_full = swap_halves(right_factor, 1)
    eye = jnp.eye(row_count, dtype=jnp.bfloat16)
    upstream_t = jnp.einsum(
        "rc,rs->cs", cotangent, eye, preferred_element_type=jnp.float32
    ).astype(jnp.bfloat16)
    upstream_t = with_layout_constraint(upstream_t, Layout((0, 1)))
    upstream_t = upstream_t.reshape(right_local, order_right, row_count)
    back_grad = jnp.einsum(
        "jmr,jkm->kjr", upstream_t, right_full, preferred_element_type=jnp.float32
    ).astype(jnp.bfloat16)
    back_sent = back_grad.reshape(peer_count, local_blocks, right_local, row_count)
    back_got = lax.all_to_all(back_sent, "blk", 0, 0, tiled=True)

    unit_mask = (jnp.arange(block_size)[None, :] < session_units[:, None]).astype(jnp.bfloat16)
    inputs = units.reshape(row_count, local_blocks, block_size) * unit_mask[None]
    left_full = swap_halves(left_factor, 1)
    mixed = jnp.einsum(
        "rki,kij->jkr", inputs, left_full, preferred_element_type=jnp.float32
    ).astype(jnp.bfloat16)
    mixed_sent = mixed.reshape(peer_count, right_local, local_blocks, row_count).transpose(0, 2, 1, 3)
    mixed_sent, back_got = lax.optimization_barrier((mixed_sent, back_got))

    half_size = block_size // 2
    core = lax.axis_index("bin")
    swap = [(0, 1), (1, 0)]
    own_part = lax.dynamic_slice_in_dim(inputs, core * half_size, half_size, axis=2)
    their_part = lax.dynamic_slice_in_dim(inputs, (1 - core) * half_size, half_size, axis=2)
    partner_part = lax.ppermute(their_part, "bin", swap)
    back_t = back_got.transpose(1, 0, 2, 3).reshape(local_blocks, block_size, row_count)
    partner_back = lax.ppermute(back_t, "bin", swap)
    mixed_got = lax.all_to_all(mixed_sent, "blk", 0, 0, tiled=True)
    left_term = jnp.einsum("rki,kjr->kij", own_part, back_t, preferred_element_type=jnp.float32)
    left_term = left_term + jnp.einsum(
        "rki,kjr->kij", partner_part, partner_back, preferred_element_type=jnp.float32
    )
    grad_left = left_term.astype(jnp.bfloat16)
    grad_left, mixed_got = lax.optimization_barrier((grad_left, mixed_got))
    half_peers = peer_count // 2

    def right_of(start):
        blocks = lax.dynamic_slice_in_dim(mixed_got, start, half_peers, axis=0)
        blocks = blocks.transpose(2, 0, 1, 3).reshape(right_local, half_peers * local_blocks, row_count)
        return jnp.einsum("jkr,rjm->jkm", blocks, upstream, preferred_element_type=jnp.float32)

    got_right = lax.ppermute(right_of((1 - core) * half_peers), "bin", [(0, 1), (1, 0)])
    grad_right = (lax.optimization_barrier(right_of(core * half_peers)) + got_right).astype(
        jnp.bfloat16
    )
    return (grad_left, grad_right)


def solution(mesh):
    placed = (
        P(("grp", "bin"), "blk"),
        P(("grp", "bin"), "blk"),
        P("blk", "bin", None),
        P("blk", "bin", None),
        P(("grp", "blk")),
    )
    return jax.shard_map(
        on_device,
        mesh=mesh,
        in_specs=placed,
        out_specs=(P(("grp", "blk"), "bin", None), P(("grp", "blk"), "bin", None)),
        check_vma=False,
    )
```

```python
import jax
import jax.numpy as jnp
from jax import lax
from jax.sharding import PartitionSpec as P
from jax.experimental.layout import Layout, with_layout_constraint


def swap_halves(local, axis):
    other = lax.ppermute(local, "bin", [(0, 1), (1, 0)])
    core = lax.axis_index("bin")
    first = jnp.where(core == 0, local, other)
    second = jnp.where(core == 0, other, local)
    return jnp.concatenate([first, second], axis=axis)


def on_device(units, cotangent, left_factor, right_factor, session_units):
    row_count = units.shape[0]
    local_blocks = left_factor.shape[0]
    block_size = left_factor.shape[2]
    right_local = right_factor.shape[0]
    order_right = right_factor.shape[2]
    peer_count = lax.axis_size("blk")
    block_count = peer_count * local_blocks

    upstream = cotangent.reshape(row_count, right_local, order_right)
    right_full = swap_halves(right_factor, 1)
    eye = jnp.eye(row_count, dtype=jnp.bfloat16)
    upstream_t = jnp.einsum(
        "rc,rs->cs", cotangent, eye, preferred_element_type=jnp.float32
    ).astype(jnp.bfloat16)
    upstream_t = with_layout_constraint(upstream_t, Layout((0, 1)))
    upstream_t = upstream_t.reshape(right_local, order_right, row_count)
    back_grad = jnp.einsum(
        "jmr,jkm->kjr", upstream_t, right_full, preferred_element_type=jnp.float32
    ).astype(jnp.bfloat16)
    back_sent = back_grad.reshape(peer_count, local_blocks, right_local, row_count)
    back_got = lax.all_to_all(back_sent, "blk", 0, 0, tiled=True)

    unit_mask = (jnp.arange(block_size)[None, :] < session_units[:, None]).astype(jnp.bfloat16)
    inputs = units.reshape(row_count, local_blocks, block_size) * unit_mask[None]
    left_full = swap_halves(left_factor, 1)
    mixed = jnp.einsum(
        "rki,kij->jkr", inputs, left_full, preferred_element_type=jnp.float32
    ).astype(jnp.bfloat16)
    mixed_sent = mixed.reshape(peer_count, right_local, local_blocks, row_count).transpose(0, 2, 1, 3)
    mixed_sent, back_got = lax.optimization_barrier((mixed_sent, back_got))

    half_size = block_size // 2
    core = lax.axis_index("bin")
    swap = [(0, 1), (1, 0)]
    own_part = lax.dynamic_slice_in_dim(inputs, core * half_size, half_size, axis=2)
    their_part = lax.dynamic_slice_in_dim(inputs, (1 - core) * half_size, half_size, axis=2)
    partner_part = lax.ppermute(their_part, "bin", swap)
    back_t = back_got.transpose(1, 0, 2, 3).reshape(local_blocks, block_size, row_count)
    partner_back = lax.ppermute(back_t, "bin", swap)
    mixed_got = lax.all_to_all(mixed_sent, "blk", 0, 0, tiled=True)
    left_term = jnp.einsum("rki,kjr->kij", own_part, back_t, preferred_element_type=jnp.float32)
    left_term = left_term + jnp.einsum(
        "rki,kjr->kij", partner_part, partner_back, preferred_element_type=jnp.float32
    )
    grad_left = left_term.astype(jnp.bfloat16)
    grad_left, mixed_got = lax.optimization_barrier((grad_left, mixed_got))
    half_peers = peer_count // 2

    def right_of(start):
        blocks = lax.dynamic_slice_in_dim(mixed_got, start, half_peers, axis=0)
        blocks = blocks.transpose(2, 0, 1, 3).reshape(right_local, half_peers * local_blocks, row_count)
        return jnp.einsum("jkr,rjm->jkm", blocks, upstream, preferred_element_type=jnp.float32)

    theirs_right = right_of((1 - core) * half_peers)
    theirs_right, own_got = lax.optimization_barrier((theirs_right, mixed_got))
    got_right = lax.ppermute(theirs_right, "bin", [(0, 1), (1, 0)])
    mixed_got = own_got
    grad_right = (lax.optimization_barrier(right_of(core * half_peers)) + got_right).astype(
        jnp.bfloat16
    )
    return (grad_left, grad_right)


def solution(mesh):
    placed = (
        P(("grp", "bin"), "blk"),
        P(("grp", "bin"), "blk"),
        P("blk", "bin", None),
        P("blk", "bin", None),
        P(("grp", "blk")),
    )
    return jax.shard_map(
        on_device,
        mesh=mesh,
        in_specs=placed,
        out_specs=(P(("grp", "blk"), "bin", None), P(("grp", "blk"), "bin", None)),
        check_vma=False,
    )
```

```python
import jax
import jax.numpy as jnp
from jax import lax
from jax.sharding import PartitionSpec as P
from jax.experimental.layout import Layout, with_layout_constraint


def swap_halves(local, axis):
    other = lax.ppermute(local, "bin", [(0, 1), (1, 0)])
    core = lax.axis_index("bin")
    first = jnp.where(core == 0, local, other)
    second = jnp.where(core == 0, other, local)
    return jnp.concatenate([first, second], axis=axis)


def on_device(units, cotangent, left_factor, right_factor, session_units):
    row_count = units.shape[0]
    local_blocks = left_factor.shape[0]
    block_size = left_factor.shape[2]
    right_local = right_factor.shape[0]
    order_right = right_factor.shape[2]
    peer_count = lax.axis_size("blk")
    block_count = peer_count * local_blocks

    upstream = cotangent.reshape(row_count, right_local, order_right)
    right_full = swap_halves(right_factor, 1)
    eye = jnp.eye(row_count, dtype=jnp.bfloat16)
    upstream_t = jnp.einsum(
        "rc,rs->cs", cotangent, eye, preferred_element_type=jnp.float32
    ).astype(jnp.bfloat16)
    upstream_t = with_layout_constraint(upstream_t, Layout((0, 1)))
    upstream_t = upstream_t.reshape(right_local, order_right, row_count)
    back_grad = jnp.einsum(
        "jmr,jkm->kjr", upstream_t, right_full, preferred_element_type=jnp.float32
    ).astype(jnp.bfloat16)
    back_sent = back_grad.reshape(peer_count, local_blocks, right_local, row_count)
    back_got = lax.all_to_all(back_sent, "blk", 0, 0, tiled=True)

    unit_mask = (jnp.arange(block_size)[None, :] < session_units[:, None]).astype(jnp.bfloat16)
    inputs = units.reshape(row_count, local_blocks, block_size) * unit_mask[None]
    left_full = swap_halves(left_factor, 1)
    mixed = jnp.einsum(
        "rki,kij->jkr", inputs, left_full, preferred_element_type=jnp.float32
    ).astype(jnp.bfloat16)
    mixed_sent = mixed.reshape(peer_count, right_local, local_blocks, row_count).transpose(0, 2, 1, 3)
    mixed_sent, back_got = lax.optimization_barrier((mixed_sent, back_got))

    half_size = block_size // 2
    core = lax.axis_index("bin")
    swap = [(0, 1), (1, 0)]
    own_part = lax.dynamic_slice_in_dim(inputs, core * half_size, half_size, axis=2)
    their_part = lax.dynamic_slice_in_dim(inputs, (1 - core) * half_size, half_size, axis=2)
    partner_part = lax.ppermute(their_part, "bin", swap)
    back_t = back_got.transpose(1, 0, 2, 3).reshape(local_blocks, block_size, row_count)
    partner_back = lax.ppermute(back_t, "bin", swap)
    mixed_got = lax.all_to_all(mixed_sent, "blk", 0, 0, tiled=True)
    left_term = jnp.einsum("rki,kjr->kij", own_part, back_t, preferred_element_type=jnp.float32)
    left_term = left_term + jnp.einsum(
        "rki,kjr->kij", partner_part, partner_back, preferred_element_type=jnp.float32
    )
    grad_left = left_term.astype(jnp.bfloat16)
    grad_left, mixed_got = lax.optimization_barrier((grad_left, mixed_got))
    half_peers = peer_count // 2
    partner_up = lax.ppermute(upstream, "bin", swap)

    def right_of(got, rows):
        blocks = got.transpose(2, 0, 1, 3).reshape(right_local, half_peers * local_blocks, row_count)
        return jnp.einsum("jkr,rjm->jkm", blocks, rows, preferred_element_type=jnp.float32)

    own_blocks = lax.dynamic_slice_in_dim(mixed_got, core * half_peers, half_peers, axis=0)
    their_blocks = lax.dynamic_slice_in_dim(mixed_got, (1 - core) * half_peers, half_peers, axis=0)
    partner_blocks = lax.ppermute(their_blocks, "bin", swap)
    own_term = lax.optimization_barrier(right_of(own_blocks, upstream))
    grad_right = (own_term + right_of(partner_blocks, partner_up)).astype(jnp.bfloat16)
    return (grad_left, grad_right)


def solution(mesh):
    placed = (
        P(("grp", "bin"), "blk"),
        P(("grp", "bin"), "blk"),
        P("blk", "bin", None),
        P("blk", "bin", None),
        P(("grp", "blk")),
    )
    return jax.shard_map(
        on_device,
        mesh=mesh,
        in_specs=placed,
        out_specs=(P(("grp", "blk"), "bin", None), P(("grp", "blk"), "bin", None)),
        check_vma=False,
    )
```

```python
import jax
import jax.numpy as jnp
from jax import lax
from jax.sharding import PartitionSpec as P
from jax.experimental.layout import Layout, with_layout_constraint


def swap_halves(local, axis):
    other = lax.ppermute(local, "bin", [(0, 1), (1, 0)])
    core = lax.axis_index("bin")
    first = jnp.where(core == 0, local, other)
    second = jnp.where(core == 0, other, local)
    return jnp.concatenate([first, second], axis=axis)


def on_device(units, cotangent, left_factor, right_factor, session_units):
    row_count = units.shape[0]
    local_blocks = left_factor.shape[0]
    block_size = left_factor.shape[2]
    right_local = right_factor.shape[0]
    order_right = right_factor.shape[2]
    peer_count = lax.axis_size("blk")
    block_count = peer_count * local_blocks

    upstream = cotangent.reshape(row_count, right_local, order_right)
    right_full = swap_halves(right_factor, 1)
    eye = jnp.eye(row_count, dtype=jnp.bfloat16)
    upstream_t = jnp.einsum(
        "rc,rs->cs", cotangent, eye, preferred_element_type=jnp.float32
    ).astype(jnp.bfloat16)
    upstream_t = with_layout_constraint(upstream_t, Layout((0, 1)))
    upstream_t = upstream_t.reshape(right_local, order_right, row_count)
    back_grad = jnp.einsum(
        "jmr,jkm->kjr", upstream_t, right_full, preferred_element_type=jnp.float32
    ).astype(jnp.bfloat16)
    back_sent = back_grad.reshape(peer_count, local_blocks, right_local, row_count)
    back_got = lax.all_to_all(back_sent, "blk", 0, 0, tiled=True)

    unit_mask = (jnp.arange(block_size)[None, :] < session_units[:, None]).astype(jnp.bfloat16)
    inputs = units.reshape(row_count, local_blocks, block_size) * unit_mask[None]
    left_full = swap_halves(left_factor, 1)
    mixed = jnp.einsum(
        "rki,kij->jkr", inputs, left_full, preferred_element_type=jnp.float32
    ).astype(jnp.bfloat16)
    mixed_sent = mixed.reshape(peer_count, right_local, local_blocks, row_count)
    mixed_sent, back_got = lax.optimization_barrier((mixed_sent, back_got))

    half_size = block_size // 2
    core = lax.axis_index("bin")
    swap = [(0, 1), (1, 0)]
    own_part = lax.dynamic_slice_in_dim(inputs, core * half_size, half_size, axis=2)
    their_part = lax.dynamic_slice_in_dim(inputs, (1 - core) * half_size, half_size, axis=2)
    partner_part = lax.ppermute(their_part, "bin", swap)
    back_t = back_got.transpose(1, 0, 2, 3).reshape(local_blocks, block_size, row_count)
    partner_back = lax.ppermute(back_t, "bin", swap)
    mixed_sent = with_layout_constraint(mixed_sent, Layout((0, 1, 2, 3)))
    mixed_got = lax.all_to_all(mixed_sent, "blk", 0, 0, tiled=True)
    mixed_got = with_layout_constraint(mixed_got, Layout((0, 1, 2, 3)))
    left_term = jnp.einsum("rki,kjr->kij", own_part, back_t, preferred_element_type=jnp.float32)
    left_term = left_term + jnp.einsum(
        "rki,kjr->kij", partner_part, partner_back, preferred_element_type=jnp.float32
    )
    grad_left = left_term.astype(jnp.bfloat16)
    grad_left, mixed_got = lax.optimization_barrier((grad_left, mixed_got))
    half_peers = peer_count // 2

    def right_of(start):
        parts = [
            jnp.einsum(
                "jkr,jmr->jkm",
                lax.dynamic_index_in_dim(mixed_got, start + q, 0, keepdims=False),
                upstream_t,
                preferred_element_type=jnp.float32,
            )
            for q in range(half_peers)
        ]
        return jnp.concatenate(parts, axis=1)

    got_right = lax.ppermute(right_of((1 - core) * half_peers), "bin", [(0, 1), (1, 0)])
    grad_right = (lax.optimization_barrier(right_of(core * half_peers)) + got_right).astype(
        jnp.bfloat16
    )
    return (grad_left, grad_right)


def solution(mesh):
    placed = (
        P(("grp", "bin"), "blk"),
        P(("grp", "bin"), "blk"),
        P("blk", "bin", None),
        P("blk", "bin", None),
        P(("grp", "blk")),
    )
    return jax.shard_map(
        on_device,
        mesh=mesh,
        in_specs=placed,
        out_specs=(P(("grp", "blk"), "bin", None), P(("grp", "blk"), "bin", None)),
        check_vma=False,
    )
```

```python
import jax
import jax.numpy as jnp
from jax import lax
from jax.sharding import PartitionSpec as P
from jax.experimental.layout import Layout, with_layout_constraint


def swap_halves(local, axis):
    other = lax.ppermute(local, "bin", [(0, 1), (1, 0)])
    core = lax.axis_index("bin")
    first = jnp.where(core == 0, local, other)
    second = jnp.where(core == 0, other, local)
    return jnp.concatenate([first, second], axis=axis)


def on_device(units, cotangent, left_factor, right_factor, session_units):
    row_count = units.shape[0]
    local_blocks = left_factor.shape[0]
    block_size = left_factor.shape[2]
    right_local = right_factor.shape[0]
    order_right = right_factor.shape[2]
    peer_count = lax.axis_size("blk")
    block_count = peer_count * local_blocks

    upstream = cotangent.reshape(row_count, right_local, order_right)
    right_full = swap_halves(right_factor, 1)
    eye = jnp.eye(row_count, dtype=jnp.bfloat16)
    upstream_t = jnp.einsum(
        "rc,rs->cs", cotangent, eye, preferred_element_type=jnp.float32
    ).astype(jnp.bfloat16)
    upstream_t = with_layout_constraint(upstream_t, Layout((0, 1)))
    upstream_t = upstream_t.reshape(right_local, order_right, row_count)
    back_grad = jnp.einsum(
        "jmr,jkm->kjr", upstream_t, right_full, preferred_element_type=jnp.float32
    ).astype(jnp.bfloat16)
    back_sent = back_grad.reshape(peer_count, local_blocks, right_local, row_count)
    back_got = lax.all_to_all(back_sent, "blk", 0, 0, tiled=True)

    unit_mask = (jnp.arange(block_size)[None, :] < session_units[:, None]).astype(jnp.bfloat16)
    inputs = units.reshape(row_count, local_blocks, block_size) * unit_mask[None]
    left_full = swap_halves(left_factor, 1)
    mixed = jnp.einsum(
        "rki,kij->jkr", inputs, left_full, preferred_element_type=jnp.float32
    ).astype(jnp.bfloat16)
    mixed_sent = mixed.reshape(peer_count, right_local, local_blocks, row_count)
    mixed_sent, back_got = lax.optimization_barrier((mixed_sent, back_got))

    half_size = block_size // 2
    core = lax.axis_index("bin")
    swap = [(0, 1), (1, 0)]
    own_part = lax.dynamic_slice_in_dim(inputs, core * half_size, half_size, axis=2)
    their_part = lax.dynamic_slice_in_dim(inputs, (1 - core) * half_size, half_size, axis=2)
    partner_part = lax.ppermute(their_part, "bin", swap)
    back_t = back_got.transpose(1, 0, 2, 3).reshape(local_blocks, block_size, row_count)
    partner_back = lax.ppermute(back_t, "bin", swap)
    mixed_sent = with_layout_constraint(mixed_sent, Layout((0, 1, 2, 3)))
    mixed_got = lax.all_to_all(mixed_sent, "blk", 0, 0, tiled=True)
    mixed_got = with_layout_constraint(mixed_got, Layout((0, 1, 2, 3)))
    left_term = jnp.einsum("rki,kjr->kij", own_part, back_t, preferred_element_type=jnp.float32)
    left_term = left_term + jnp.einsum(
        "rki,kjr->kij", partner_part, partner_back, preferred_element_type=jnp.float32
    )
    grad_left = left_term.astype(jnp.bfloat16)
    grad_left, mixed_got = lax.optimization_barrier((grad_left, mixed_got))
    half_peers = peer_count // 2

    def right_of(start):
        blocks = lax.dynamic_slice_in_dim(mixed_got, start, half_peers, axis=0)
        blocks = blocks.transpose(1, 0, 2, 3).reshape(right_local, half_peers * local_blocks, row_count)
        return jnp.einsum("jkr,rjm->jkm", blocks, upstream, preferred_element_type=jnp.float32)

    got_right = lax.ppermute(right_of((1 - core) * half_peers), "bin", [(0, 1), (1, 0)])
    grad_right = (lax.optimization_barrier(right_of(core * half_peers)) + got_right).astype(
        jnp.bfloat16
    )
    return (grad_left, grad_right)


def solution(mesh):
    placed = (
        P(("grp", "bin"), "blk"),
        P(("grp", "bin"), "blk"),
        P("blk", "bin", None),
        P("blk", "bin", None),
        P(("grp", "blk")),
    )
    return jax.shard_map(
        on_device,
        mesh=mesh,
        in_specs=placed,
        out_specs=(P(("grp", "blk"), "bin", None), P(("grp", "blk"), "bin", None)),
        check_vma=False,
    )
```

```python
import jax
import jax.numpy as jnp
from jax import lax
from jax.sharding import PartitionSpec as P
from jax.experimental.layout import Layout, with_layout_constraint


def swap_halves(local, axis):
    other = lax.ppermute(local, "bin", [(0, 1), (1, 0)])
    core = lax.axis_index("bin")
    first = jnp.where(core == 0, local, other)
    second = jnp.where(core == 0, other, local)
    return jnp.concatenate([first, second], axis=axis)


def on_device(units, cotangent, left_factor, right_factor, session_units):
    row_count = units.shape[0]
    local_blocks = left_factor.shape[0]
    block_size = left_factor.shape[2]
    right_local = right_factor.shape[0]
    order_right = right_factor.shape[2]
    peer_count = lax.axis_size("blk")
    block_count = peer_count * local_blocks

    upstream = cotangent.reshape(row_count, right_local, order_right)
    right_full = swap_halves(right_factor, 1)
    eye = jnp.eye(row_count, dtype=jnp.bfloat16)
    upstream_t = jnp.einsum(
        "rc,rs->cs", cotangent, eye, preferred_element_type=jnp.float32
    ).astype(jnp.bfloat16)
    upstream_t = with_layout_constraint(upstream_t, Layout((0, 1)))
    upstream_t = upstream_t.reshape(right_local, order_right, row_count)
    back_grad = jnp.einsum(
        "jmr,jkm->kjr", upstream_t, right_full, preferred_element_type=jnp.float32
    ).astype(jnp.bfloat16)
    back_sent = back_grad.reshape(peer_count, local_blocks, right_local, row_count)
    back_got = lax.all_to_all(back_sent, "blk", 0, 0, tiled=True)

    unit_mask = (jnp.arange(block_size)[None, :] < session_units[:, None]).astype(jnp.bfloat16)
    inputs = units.reshape(row_count, local_blocks, block_size) * unit_mask[None]
    half_rows = block_size // 2
    core_here = lax.axis_index("bin")
    left_other = lax.ppermute(left_factor, "bin", [(0, 1), (1, 0)])
    own_inputs = lax.dynamic_slice_in_dim(inputs, core_here * half_rows, half_rows, axis=2)
    other_inputs = lax.dynamic_slice_in_dim(inputs, (1 - core_here) * half_rows, half_rows, axis=2)
    mixed = (
        jnp.einsum("rki,kij->jkr", own_inputs, left_factor, preferred_element_type=jnp.float32)
        + jnp.einsum("rki,kij->jkr", other_inputs, left_other, preferred_element_type=jnp.float32)
    ).astype(jnp.bfloat16)
    mixed_sent = mixed.reshape(peer_count, right_local, local_blocks, row_count)
    mixed_sent, back_got = lax.optimization_barrier((mixed_sent, back_got))

    half_size = block_size // 2
    core = lax.axis_index("bin")
    swap = [(0, 1), (1, 0)]
    own_part = lax.dynamic_slice_in_dim(inputs, core * half_size, half_size, axis=2)
    their_part = lax.dynamic_slice_in_dim(inputs, (1 - core) * half_size, half_size, axis=2)
    partner_part = lax.ppermute(their_part, "bin", swap)
    back_t = back_got.transpose(1, 0, 2, 3).reshape(local_blocks, block_size, row_count)
    partner_back = lax.ppermute(back_t, "bin", swap)
    mixed_sent = with_layout_constraint(mixed_sent, Layout((0, 1, 2, 3)))
    mixed_got = lax.all_to_all(mixed_sent, "blk", 0, 0, tiled=True)
    mixed_got = with_layout_constraint(mixed_got, Layout((0, 1, 2, 3)))
    left_term = jnp.einsum("rki,kjr->kij", own_part, back_t, preferred_element_type=jnp.float32)
    left_term = left_term + jnp.einsum(
        "rki,kjr->kij", partner_part, partner_back, preferred_element_type=jnp.float32
    )
    grad_left = left_term.astype(jnp.bfloat16)
    grad_left, mixed_got = lax.optimization_barrier((grad_left, mixed_got))
    half_peers = peer_count // 2

    def right_of(start):
        blocks = lax.dynamic_slice_in_dim(mixed_got, start, half_peers, axis=0)
        blocks = blocks.transpose(1, 0, 2, 3).reshape(right_local, half_peers * local_blocks, row_count)
        return jnp.einsum("jkr,rjm->jkm", blocks, upstream, preferred_element_type=jnp.float32)

    got_right = lax.ppermute(right_of((1 - core) * half_peers), "bin", [(0, 1), (1, 0)])
    grad_right = (lax.optimization_barrier(right_of(core * half_peers)) + got_right).astype(
        jnp.bfloat16
    )
    return (grad_left, grad_right)


def solution(mesh):
    placed = (
        P(("grp", "bin"), "blk"),
        P(("grp", "bin"), "blk"),
        P("blk", "bin", None),
        P("blk", "bin", None),
        P(("grp", "blk")),
    )
    return jax.shard_map(
        on_device,
        mesh=mesh,
        in_specs=placed,
        out_specs=(P(("grp", "blk"), "bin", None), P(("grp", "blk"), "bin", None)),
        check_vma=False,
    )
```

```python
import jax
import jax.numpy as jnp
from jax import lax
from jax.sharding import PartitionSpec as P
from jax.experimental.layout import Layout, with_layout_constraint


def swap_halves(local, axis):
    other = lax.ppermute(local, "bin", [(0, 1), (1, 0)])
    core = lax.axis_index("bin")
    first = jnp.where(core == 0, local, other)
    second = jnp.where(core == 0, other, local)
    return jnp.concatenate([first, second], axis=axis)


def on_device(units, cotangent, left_factor, right_factor, session_units):
    row_count = units.shape[0]
    local_blocks = left_factor.shape[0]
    block_size = left_factor.shape[2]
    right_local = right_factor.shape[0]
    order_right = right_factor.shape[2]
    peer_count = lax.axis_size("blk")
    block_count = peer_count * local_blocks

    upstream = cotangent.reshape(row_count, right_local, order_right)
    right_full = swap_halves(right_factor, 1)
    eye = jnp.eye(row_count, dtype=jnp.bfloat16)
    upstream_t = jnp.einsum(
        "rc,rs->cs", cotangent, eye, preferred_element_type=jnp.float32
    ).astype(jnp.bfloat16)
    upstream_t = with_layout_constraint(upstream_t, Layout((0, 1)))
    upstream_t = upstream_t.reshape(right_local, order_right, row_count)
    back_grad = jnp.einsum(
        "jmr,jkm->kjr", upstream_t, right_full, preferred_element_type=jnp.float32
    ).astype(jnp.bfloat16)
    back_sent = back_grad.reshape(peer_count, local_blocks, right_local, row_count)
    back_got = lax.all_to_all(back_sent, "blk", 0, 0, tiled=True)

    unit_mask = (jnp.arange(block_size)[None, :] < session_units[:, None]).astype(jnp.bfloat16)
    inputs = units.reshape(row_count, local_blocks, block_size) * unit_mask[None]
    left_full = swap_halves(left_factor, 1)
    mixed = jnp.einsum(
        "rki,kij->jkr", inputs, left_full, preferred_element_type=jnp.float32
    ).astype(jnp.bfloat16)
    mixed_sent = mixed.reshape(peer_count, right_local, local_blocks, row_count)
    mixed_sent, back_got = lax.optimization_barrier((mixed_sent, back_got))

    half_size = block_size // 2
    core = lax.axis_index("bin")
    swap = [(0, 1), (1, 0)]
    own_part = lax.dynamic_slice_in_dim(inputs, core * half_size, half_size, axis=2)
    their_part = lax.dynamic_slice_in_dim(inputs, (1 - core) * half_size, half_size, axis=2)
    partner_part = lax.ppermute(their_part, "bin", swap)
    back_t = back_got.transpose(1, 0, 2, 3).reshape(local_blocks, block_size, row_count)
    partner_back = lax.ppermute(back_t, "bin", swap)
    mixed_sent = with_layout_constraint(mixed_sent, Layout((0, 1, 2, 3)))
    mixed_got = lax.all_to_all(mixed_sent, "blk", 0, 0, tiled=True)
    mixed_got = with_layout_constraint(mixed_got, Layout((0, 1, 2, 3)))
    left_term = jnp.einsum("rki,kjr->kij", own_part, back_t, preferred_element_type=jnp.float32)
    left_term = left_term + jnp.einsum(
        "rki,kjr->kij", partner_part, partner_back, preferred_element_type=jnp.float32
    )
    grad_left = left_term.astype(jnp.bfloat16)
    grad_left, mixed_got = lax.optimization_barrier((grad_left, mixed_got))
    half_peers = peer_count // 2

    def right_of(start, j_start, j_count):
        blocks = lax.dynamic_slice_in_dim(mixed_got, start, half_peers, axis=0)[:, j_start:j_start + j_count]
        blocks = blocks.transpose(1, 0, 2, 3).reshape(j_count, half_peers * local_blocks, row_count)
        rows = upstream[:, j_start:j_start + j_count]
        return jnp.einsum("jkr,rjm->jkm", blocks, rows, preferred_element_type=jnp.float32)

    half_j = right_local // 2
    got_right = jnp.concatenate(
        [
            lax.ppermute(right_of((1 - core) * half_peers, j0, half_j), "bin", [(0, 1), (1, 0)])
            for j0 in (0, half_j)
        ],
        axis=0,
    )
    own_right = lax.optimization_barrier(right_of(core * half_peers, 0, right_local))
    grad_right = (own_right + got_right).astype(jnp.bfloat16)
    return (grad_left, grad_right)


def solution(mesh):
    placed = (
        P(("grp", "bin"), "blk"),
        P(("grp", "bin"), "blk"),
        P("blk", "bin", None),
        P("blk", "bin", None),
        P(("grp", "blk")),
    )
    return jax.shard_map(
        on_device,
        mesh=mesh,
        in_specs=placed,
        out_specs=(P(("grp", "blk"), "bin", None), P(("grp", "blk"), "bin", None)),
        check_vma=False,
    )
```

```python
import jax
import jax.numpy as jnp
from jax import lax
from jax.sharding import PartitionSpec as P
from jax.experimental.layout import Layout, with_layout_constraint


def swap_halves(local, axis):
    other = lax.ppermute(local, "bin", [(0, 1), (1, 0)])
    core = lax.axis_index("bin")
    first = jnp.where(core == 0, local, other)
    second = jnp.where(core == 0, other, local)
    return jnp.concatenate([first, second], axis=axis)


def on_device(units, cotangent, left_factor, right_factor, session_units):
    row_count = units.shape[0]
    local_blocks = left_factor.shape[0]
    block_size = left_factor.shape[2]
    right_local = right_factor.shape[0]
    order_right = right_factor.shape[2]
    peer_count = lax.axis_size("blk")
    block_count = peer_count * local_blocks

    upstream = cotangent.reshape(row_count, right_local, order_right)
    right_full = swap_halves(right_factor, 1)
    eye = jnp.eye(row_count, dtype=jnp.bfloat16)
    upstream_t = jnp.einsum(
        "rc,rs->cs", cotangent, eye, preferred_element_type=jnp.float32
    ).astype(jnp.bfloat16)
    upstream_t = with_layout_constraint(upstream_t, Layout((0, 1)))
    upstream_t = upstream_t.reshape(right_local, order_right, row_count)
    back_grad = jnp.einsum(
        "jmr,jkm->kjr", upstream_t, right_full, preferred_element_type=jnp.float32
    ).astype(jnp.bfloat16)
    back_sent = back_grad.reshape(peer_count, local_blocks, right_local, row_count)
    back_got = lax.all_to_all(back_sent, "blk", 0, 0, tiled=True)

    unit_mask = (jnp.arange(block_size)[None, :] < session_units[:, None]).astype(jnp.bfloat16)
    inputs = units.reshape(row_count, local_blocks, block_size) * unit_mask[None]
    left_full = swap_halves(left_factor, 1)
    mixed = jnp.einsum(
        "rki,kij->jkr", inputs, left_full, preferred_element_type=jnp.float32
    ).astype(jnp.bfloat16)
    mixed_sent = mixed.reshape(peer_count, right_local, local_blocks, row_count)
    mixed_sent, back_got = lax.optimization_barrier((mixed_sent, back_got))

    half_size = block_size // 2
    core = lax.axis_index("bin")
    swap = [(0, 1), (1, 0)]
    own_part = lax.dynamic_slice_in_dim(inputs, core * half_size, half_size, axis=2)
    their_part = lax.dynamic_slice_in_dim(inputs, (1 - core) * half_size, half_size, axis=2)
    partner_part = lax.ppermute(their_part, "bin", swap)
    back_t = back_got.transpose(1, 0, 2, 3).reshape(local_blocks, block_size, row_count)
    partner_back = lax.ppermute(back_t, "bin", swap)
    mixed_sent = with_layout_constraint(mixed_sent, Layout((0, 1, 2, 3)))
    mixed_got = lax.all_to_all(mixed_sent, "blk", 0, 0, tiled=True)
    mixed_got = with_layout_constraint(mixed_got, Layout((0, 1, 2, 3)))
    left_term = jnp.einsum("rki,kjr->kij", own_part, back_t, preferred_element_type=jnp.float32)
    left_term = left_term + jnp.einsum(
        "rki,kjr->kij", partner_part, partner_back, preferred_element_type=jnp.float32
    )
    grad_left = left_term.astype(jnp.bfloat16)
    grad_left, mixed_got = lax.optimization_barrier((grad_left, mixed_got))
    half_peers = peer_count // 2

    def right_of(start, j_start, j_count):
        blocks = lax.dynamic_slice_in_dim(mixed_got, start, half_peers, axis=0)[:, j_start:j_start + j_count]
        blocks = blocks.transpose(1, 0, 2, 3).reshape(j_count, half_peers * local_blocks, row_count)
        rows = upstream[:, j_start:j_start + j_count]
        return jnp.einsum("jkr,rjm->jkm", blocks, rows, preferred_element_type=jnp.float32)

    half_j = right_local // 2
    got_right = jnp.concatenate(
        [
            lax.ppermute(right_of((1 - core) * half_peers, j0, half_j), "bin", [(0, 1), (1, 0)])
            for j0 in (0, half_j)
        ],
        axis=0,
    )
    grad_right = (right_of(core * half_peers, 0, right_local) + got_right).astype(jnp.bfloat16)
    return (grad_left, grad_right)


def solution(mesh):
    placed = (
        P(("grp", "bin"), "blk"),
        P(("grp", "bin"), "blk"),
        P("blk", "bin", None),
        P("blk", "bin", None),
        P(("grp", "blk")),
    )
    return jax.shard_map(
        on_device,
        mesh=mesh,
        in_specs=placed,
        out_specs=(P(("grp", "blk"), "bin", None), P(("grp", "blk"), "bin", None)),
        check_vma=False,
    )
```

```python
import jax
import jax.numpy as jnp
from jax import lax
from jax.sharding import PartitionSpec as P
from jax.experimental.layout import Layout, with_layout_constraint


def swap_halves(local, axis):
    other = lax.ppermute(local, "bin", [(0, 1), (1, 0)])
    core = lax.axis_index("bin")
    first = jnp.where(core == 0, local, other)
    second = jnp.where(core == 0, other, local)
    return jnp.concatenate([first, second], axis=axis)


def on_device(units, cotangent, left_factor, right_factor, session_units):
    row_count = units.shape[0]
    local_blocks = left_factor.shape[0]
    block_size = left_factor.shape[2]
    right_local = right_factor.shape[0]
    order_right = right_factor.shape[2]
    peer_count = lax.axis_size("blk")
    block_count = peer_count * local_blocks

    upstream = cotangent.reshape(row_count, right_local, order_right)
    right_full = swap_halves(right_factor, 1)
    eye = jnp.eye(row_count, dtype=jnp.bfloat16)
    upstream_t = jnp.einsum(
        "rc,rs->cs", cotangent, eye, preferred_element_type=jnp.float32
    ).astype(jnp.bfloat16)
    upstream_t = with_layout_constraint(upstream_t, Layout((0, 1)))
    upstream_t = upstream_t.reshape(right_local, order_right, row_count)
    back_grad = jnp.einsum(
        "jmr,jkm->kjr", upstream_t, right_full, preferred_element_type=jnp.float32
    ).astype(jnp.bfloat16)
    back_sent = back_grad.reshape(peer_count, local_blocks, right_local, row_count)
    back_got = lax.all_to_all(back_sent, "blk", 0, 0, tiled=True)

    unit_mask = (jnp.arange(block_size)[None, :] < session_units[:, None]).astype(jnp.bfloat16)
    inputs = units.reshape(row_count, local_blocks, block_size) * unit_mask[None]
    left_full = swap_halves(left_factor, 1)
    mixed = jnp.einsum(
        "rki,kij->jkr", inputs, left_full, preferred_element_type=jnp.float32
    ).astype(jnp.bfloat16)
    mixed_sent = mixed.reshape(peer_count, right_local, local_blocks, row_count)
    mixed_sent, back_got = lax.optimization_barrier((mixed_sent, back_got))

    half_size = block_size // 2
    core = lax.axis_index("bin")
    swap = [(0, 1), (1, 0)]
    own_part = lax.dynamic_slice_in_dim(inputs, core * half_size, half_size, axis=2)
    their_part = lax.dynamic_slice_in_dim(inputs, (1 - core) * half_size, half_size, axis=2)
    partner_part = lax.ppermute(their_part, "bin", swap)
    back_t = back_got.transpose(1, 0, 2, 3).reshape(local_blocks, block_size, row_count)
    partner_back = lax.ppermute(back_t, "bin", swap)
    mixed_sent = with_layout_constraint(mixed_sent, Layout((0, 1, 2, 3)))
    mixed_got = lax.all_to_all(mixed_sent, "blk", 0, 0, tiled=True)
    mixed_got = with_layout_constraint(mixed_got, Layout((0, 1, 2, 3)))
    left_term = jnp.einsum("rki,kjr->kij", own_part, back_t, preferred_element_type=jnp.float32)
    left_term = left_term + jnp.einsum(
        "rki,kjr->kij", partner_part, partner_back, preferred_element_type=jnp.float32
    )
    grad_left = left_term.astype(jnp.bfloat16)
    grad_left, mixed_got = lax.optimization_barrier((grad_left, mixed_got))
    half_peers = peer_count // 2

    def right_of(start, j_start, j_count):
        blocks = lax.dynamic_slice_in_dim(mixed_got, start, half_peers, axis=0)[:, j_start:j_start + j_count]
        blocks = blocks.transpose(1, 0, 2, 3).reshape(j_count, half_peers * local_blocks, row_count)
        rows = upstream[:, j_start:j_start + j_count]
        return jnp.einsum("jkr,rjm->jkm", blocks, rows, preferred_element_type=jnp.float32)

    half_j = right_local // 2
    sent_right = [right_of((1 - core) * half_peers, j0, half_j) for j0 in (0, half_j)]
    sent_right, mixed_got = lax.optimization_barrier((sent_right, mixed_got))
    got_right = jnp.concatenate(
        [lax.ppermute(part, "bin", [(0, 1), (1, 0)]) for part in sent_right], axis=0
    )
    own_right = lax.optimization_barrier(right_of(core * half_peers, 0, right_local))
    grad_right = (own_right + got_right).astype(jnp.bfloat16)
    return (grad_left, grad_right)


def solution(mesh):
    placed = (
        P(("grp", "bin"), "blk"),
        P(("grp", "bin"), "blk"),
        P("blk", "bin", None),
        P("blk", "bin", None),
        P(("grp", "blk")),
    )
    return jax.shard_map(
        on_device,
        mesh=mesh,
        in_specs=placed,
        out_specs=(P(("grp", "blk"), "bin", None), P(("grp", "blk"), "bin", None)),
        check_vma=False,
    )
```

```python
import jax
import jax.numpy as jnp
from jax import lax
from jax.sharding import PartitionSpec as P
from jax.experimental import pallas as pl
from jax.experimental.pallas import tpu as pltpu
from jax.experimental.layout import Layout, with_layout_constraint


def _transpose_kernel(x_ref, o_ref):
    width = 128

    def body(step, carry):
        start = pl.multiple_of(step * width, width)
        o_ref[pl.ds(start, width), :] = x_ref[:, pl.ds(start, width)].T
        return carry

    lax.fori_loop(0, x_ref.shape[1] // width, body, 0)


def transposed(x):
    rows, cols = x.shape
    return pl.pallas_call(
        _transpose_kernel,
        out_shape=jax.ShapeDtypeStruct((cols, rows), x.dtype),
        in_specs=[pl.BlockSpec(memory_space=pltpu.VMEM)],
        out_specs=pl.BlockSpec(memory_space=pltpu.VMEM),
        cost_estimate=pl.CostEstimate(flops=0, bytes_accessed=2 * x.size * x.dtype.itemsize, transcendentals=0),
    )(x)


def swap_halves(local, axis):
    other = lax.ppermute(local, "bin", [(0, 1), (1, 0)])
    core = lax.axis_index("bin")
    first = jnp.where(core == 0, local, other)
    second = jnp.where(core == 0, other, local)
    return jnp.concatenate([first, second], axis=axis)


def on_device(units, cotangent, left_factor, right_factor, session_units):
    row_count = units.shape[0]
    local_blocks = left_factor.shape[0]
    block_size = left_factor.shape[2]
    right_local = right_factor.shape[0]
    order_right = right_factor.shape[2]
    peer_count = lax.axis_size("blk")
    block_count = peer_count * local_blocks

    upstream = cotangent.reshape(row_count, right_local, order_right)
    right_full = swap_halves(right_factor, 1)
    upstream_t = transposed(cotangent).reshape(right_local, order_right, row_count)
    back_grad = jnp.einsum(
        "jmr,jkm->kjr", upstream_t, right_full, preferred_element_type=jnp.float32
    ).astype(jnp.bfloat16)
    back_sent = back_grad.reshape(peer_count, local_blocks, right_local, row_count)
    back_got = lax.all_to_all(back_sent, "blk", 0, 0, tiled=True)

    unit_mask = (jnp.arange(block_size)[None, :] < session_units[:, None]).astype(jnp.bfloat16)
    inputs = units.reshape(row_count, local_blocks, block_size) * unit_mask[None]
    left_full = swap_halves(left_factor, 1)
    mixed = jnp.einsum(
        "rki,kij->jkr", inputs, left_full, preferred_element_type=jnp.float32
    ).astype(jnp.bfloat16)
    mixed_sent = mixed.reshape(peer_count, right_local, local_blocks, row_count)
    mixed_sent, back_got = lax.optimization_barrier((mixed_sent, back_got))

    half_size = block_size // 2
    core = lax.axis_index("bin")
    swap = [(0, 1), (1, 0)]
    own_part = lax.dynamic_slice_in_dim(inputs, core * half_size, half_size, axis=2)
    their_part = lax.dynamic_slice_in_dim(inputs, (1 - core) * half_size, half_size, axis=2)
    partner_part = lax.ppermute(their_part, "bin", swap)
    back_t = back_got.transpose(1, 0, 2, 3).reshape(local_blocks, block_size, row_count)
    partner_back = lax.ppermute(back_t, "bin", swap)
    mixed_sent = with_layout_constraint(mixed_sent, Layout((0, 1, 2, 3)))
    mixed_got = lax.all_to_all(mixed_sent, "blk", 0, 0, tiled=True)
    mixed_got = with_layout_constraint(mixed_got, Layout((0, 1, 2, 3)))
    left_term = jnp.einsum("rki,kjr->kij", own_part, back_t, preferred_element_type=jnp.float32)
    left_term = left_term + jnp.einsum(
        "rki,kjr->kij", partner_part, partner_back, preferred_element_type=jnp.float32
    )
    grad_left = left_term.astype(jnp.bfloat16)
    grad_left, mixed_got = lax.optimization_barrier((grad_left, mixed_got))
    half_peers = peer_count // 2

    def right_of(start, j_start, j_count):
        blocks = lax.dynamic_slice_in_dim(mixed_got, start, half_peers, axis=0)[:, j_start:j_start + j_count]
        blocks = blocks.transpose(1, 0, 2, 3).reshape(j_count, half_peers * local_blocks, row_count)
        rows = upstream[:, j_start:j_start + j_count]
        return jnp.einsum("jkr,rjm->jkm", blocks, rows, preferred_element_type=jnp.float32)

    half_j = right_local // 2
    sent_right = [right_of((1 - core) * half_peers, j0, half_j) for j0 in (0, half_j)]
    sent_right, mixed_got = lax.optimization_barrier((sent_right, mixed_got))
    got_right = jnp.concatenate(
        [lax.ppermute(part, "bin", [(0, 1), (1, 0)]) for part in sent_right], axis=0
    )
    own_right = lax.optimization_barrier(right_of(core * half_peers, 0, right_local))
    grad_right = (own_right + got_right).astype(jnp.bfloat16)
    return (grad_left, grad_right)


def solution(mesh):
    placed = (
        P(("grp", "bin"), "blk"),
        P(("grp", "bin"), "blk"),
        P("blk", "bin", None),
        P("blk", "bin", None),
        P(("grp", "blk")),
    )
    return jax.shard_map(
        on_device,
        mesh=mesh,
        in_specs=placed,
        out_specs=(P(("grp", "blk"), "bin", None), P(("grp", "blk"), "bin", None)),
        check_vma=False,
    )
```

```python
import jax
import jax.numpy as jnp
from jax import lax
from jax.sharding import PartitionSpec as P
from jax.experimental.layout import Layout, with_layout_constraint


def swap_halves(local, axis):
    other = lax.ppermute(local, "bin", [(0, 1), (1, 0)])
    core = lax.axis_index("bin")
    first = jnp.where(core == 0, local, other)
    second = jnp.where(core == 0, other, local)
    return jnp.concatenate([first, second], axis=axis)


def on_device(units, cotangent, left_factor, right_factor, session_units):
    row_count = units.shape[0]
    local_blocks = left_factor.shape[0]
    block_size = left_factor.shape[2]
    right_local = right_factor.shape[0]
    order_right = right_factor.shape[2]
    peer_count = lax.axis_size("blk")
    block_count = peer_count * local_blocks

    upstream = cotangent.reshape(row_count, right_local, order_right)
    right_full = swap_halves(right_factor, 1)
    eye = jnp.eye(row_count, dtype=jnp.bfloat16)
    upstream_t = jnp.einsum(
        "rc,rs->cs", cotangent, eye, preferred_element_type=jnp.float32
    ).astype(jnp.bfloat16)
    upstream_t = with_layout_constraint(upstream_t, Layout((0, 1)))
    upstream_t = upstream_t.reshape(right_local, order_right, row_count)
    back_grad = jnp.einsum(
        "jmr,jkm->kjr", upstream_t, right_full, preferred_element_type=jnp.float32
    ).astype(jnp.bfloat16)
    back_sent = back_grad.reshape(peer_count, local_blocks, right_local, row_count)
    back_got = lax.all_to_all(back_sent, "blk", 0, 0, tiled=True)

    unit_mask = (jnp.arange(block_size)[None, :] < session_units[:, None]).astype(jnp.bfloat16)
    inputs = units.reshape(row_count, local_blocks, block_size) * unit_mask[None]
    left_full = swap_halves(left_factor, 1)
    mixed = jnp.einsum(
        "rki,kij->jkr", inputs, left_full, preferred_element_type=jnp.float32
    ).astype(jnp.bfloat16)
    mixed_sent = mixed.reshape(peer_count, right_local, local_blocks, row_count)
    mixed_sent, back_got = lax.optimization_barrier((mixed_sent, back_got))

    half_size = block_size // 2
    core = lax.axis_index("bin")
    swap = [(0, 1), (1, 0)]
    own_part = lax.dynamic_slice_in_dim(inputs, core * half_size, half_size, axis=2)
    their_part = lax.dynamic_slice_in_dim(inputs, (1 - core) * half_size, half_size, axis=2)
    partner_part = lax.ppermute(their_part, "bin", swap)
    back_t = back_got.transpose(1, 0, 2, 3).reshape(local_blocks, block_size, row_count)
    partner_back = lax.ppermute(back_t, "bin", swap)
    mixed_sent = with_layout_constraint(mixed_sent, Layout((0, 1, 2, 3)))
    mixed_got = lax.all_to_all(mixed_sent, "blk", 0, 0, tiled=True)
    mixed_got = with_layout_constraint(mixed_got, Layout((0, 1, 2, 3)))
    left_term = jnp.einsum("rki,kjr->kij", own_part, back_t, preferred_element_type=jnp.float32)
    left_term = left_term + jnp.einsum(
        "rki,kjr->kij", partner_part, partner_back, preferred_element_type=jnp.float32
    )
    grad_left = left_term.astype(jnp.bfloat16)
    grad_left, mixed_got = lax.optimization_barrier((grad_left, mixed_got))
    half_peers = peer_count // 2

    def right_of(start, j_start, j_count):
        blocks = lax.dynamic_slice_in_dim(mixed_got, start, half_peers, axis=0)[:, j_start:j_start + j_count]
        blocks = blocks.transpose(1, 0, 2, 3).reshape(j_count, half_peers * local_blocks, row_count)
        rows = upstream[:, j_start:j_start + j_count]
        return jnp.einsum("jkr,rjm->jkm", blocks, rows, preferred_element_type=jnp.float32)

    half_j = right_local // 4 if right_local % 4 == 0 else right_local // 2
    got_right = jnp.concatenate(
        [
            lax.ppermute(right_of((1 - core) * half_peers, j0, half_j), "bin", [(0, 1), (1, 0)])
            for j0 in range(0, right_local, half_j)
        ],
        axis=0,
    )
    own_right = lax.optimization_barrier(right_of(core * half_peers, 0, right_local))
    grad_right = (own_right + got_right).astype(jnp.bfloat16)
    return (grad_left, grad_right)


def solution(mesh):
    placed = (
        P(("grp", "bin"), "blk"),
        P(("grp", "bin"), "blk"),
        P("blk", "bin", None),
        P("blk", "bin", None),
        P(("grp", "blk")),
    )
    return jax.shard_map(
        on_device,
        mesh=mesh,
        in_specs=placed,
        out_specs=(P(("grp", "blk"), "bin", None), P(("grp", "blk"), "bin", None)),
        check_vma=False,
    )
```

```python
import jax
import jax.numpy as jnp
from jax import lax
from jax.sharding import PartitionSpec as P
from jax.experimental.layout import Layout, with_layout_constraint


def swap_halves(local, axis):
    other = lax.ppermute(local, "bin", [(0, 1), (1, 0)])
    core = lax.axis_index("bin")
    first = jnp.where(core == 0, local, other)
    second = jnp.where(core == 0, other, local)
    return jnp.concatenate([first, second], axis=axis)


def on_device(units, cotangent, left_factor, right_factor, session_units):
    row_count = units.shape[0]
    local_blocks = left_factor.shape[0]
    block_size = left_factor.shape[2]
    right_local = right_factor.shape[0]
    order_right = right_factor.shape[2]
    peer_count = lax.axis_size("blk")
    block_count = peer_count * local_blocks

    upstream = cotangent.reshape(row_count, right_local, order_right)
    right_full = swap_halves(right_factor, 1)
    eye = jnp.eye(row_count, dtype=jnp.bfloat16)
    upstream_t = jnp.einsum(
        "rc,rs->cs", cotangent, eye, preferred_element_type=jnp.float32
    ).astype(jnp.bfloat16)
    upstream_t = with_layout_constraint(upstream_t, Layout((0, 1)))
    upstream_t = upstream_t.reshape(right_local, order_right, row_count)
    back_grad = jnp.einsum(
        "jmr,jkm->kjr", upstream_t, right_full, preferred_element_type=jnp.float32
    ).astype(jnp.bfloat16)
    back_sent = back_grad.reshape(peer_count, local_blocks, right_local, row_count)
    back_sent = with_layout_constraint(back_sent, Layout((0, 1, 2, 3)))
    back_got = lax.all_to_all(back_sent, "blk", 0, 0, tiled=True)

    unit_mask = (jnp.arange(block_size)[None, :] < session_units[:, None]).astype(jnp.bfloat16)
    inputs = units.reshape(row_count, local_blocks, block_size) * unit_mask[None]
    left_full = swap_halves(left_factor, 1)
    mixed = jnp.einsum(
        "rki,kij->jkr", inputs, left_full, preferred_element_type=jnp.float32
    ).astype(jnp.bfloat16)
    mixed_sent = mixed.reshape(peer_count, right_local, local_blocks, row_count)
    mixed_sent, back_got = lax.optimization_barrier((mixed_sent, back_got))

    half_size = block_size // 2
    core = lax.axis_index("bin")
    swap = [(0, 1), (1, 0)]
    own_part = lax.dynamic_slice_in_dim(inputs, core * half_size, half_size, axis=2)
    their_part = lax.dynamic_slice_in_dim(inputs, (1 - core) * half_size, half_size, axis=2)
    partner_part = lax.ppermute(their_part, "bin", swap)
    back_t = back_got.transpose(1, 0, 2, 3).reshape(local_blocks, block_size, row_count)
    partner_back = lax.ppermute(back_t, "bin", swap)
    mixed_sent = with_layout_constraint(mixed_sent, Layout((0, 1, 2, 3)))
    mixed_got = lax.all_to_all(mixed_sent, "blk", 0, 0, tiled=True)
    mixed_got = with_layout_constraint(mixed_got, Layout((0, 1, 2, 3)))
    left_term = jnp.einsum("rki,kjr->kij", own_part, back_t, preferred_element_type=jnp.float32)
    left_term = left_term + jnp.einsum(
        "rki,kjr->kij", partner_part, partner_back, preferred_element_type=jnp.float32
    )
    grad_left = left_term.astype(jnp.bfloat16)
    grad_left, mixed_got = lax.optimization_barrier((grad_left, mixed_got))
    half_peers = peer_count // 2

    def right_of(start, j_start, j_count):
        blocks = lax.dynamic_slice_in_dim(mixed_got, start, half_peers, axis=0)[:, j_start:j_start + j_count]
        blocks = blocks.transpose(1, 0, 2, 3).reshape(j_count, half_peers * local_blocks, row_count)
        rows = upstream[:, j_start:j_start + j_count]
        return jnp.einsum("jkr,rjm->jkm", blocks, rows, preferred_element_type=jnp.float32)

    half_j = right_local // 2
    sent_right = [right_of((1 - core) * half_peers, j0, half_j) for j0 in (0, half_j)]
    sent_right, mixed_got = lax.optimization_barrier((sent_right, mixed_got))
    got_right = jnp.concatenate(
        [lax.ppermute(part, "bin", [(0, 1), (1, 0)]) for part in sent_right], axis=0
    )
    own_right = lax.optimization_barrier(right_of(core * half_peers, 0, right_local))
    grad_right = (own_right + got_right).astype(jnp.bfloat16)
    return (grad_left, grad_right)


def solution(mesh):
    placed = (
        P(("grp", "bin"), "blk"),
        P(("grp", "bin"), "blk"),
        P("blk", "bin", None),
        P("blk", "bin", None),
        P(("grp", "blk")),
    )
    return jax.shard_map(
        on_device,
        mesh=mesh,
        in_specs=placed,
        out_specs=(P(("grp", "blk"), "bin", None), P(("grp", "blk"), "bin", None)),
        check_vma=False,
    )
```

```python
import jax
import jax.numpy as jnp
from jax import lax
from jax.sharding import PartitionSpec as P
from jax.experimental.layout import Layout, with_layout_constraint


def swap_halves(local, axis):
    other = lax.ppermute(local, "bin", [(0, 1), (1, 0)])
    core = lax.axis_index("bin")
    first = jnp.where(core == 0, local, other)
    second = jnp.where(core == 0, other, local)
    return jnp.concatenate([first, second], axis=axis)


def on_device(units, cotangent, left_factor, right_factor, session_units):
    row_count = units.shape[0]
    local_blocks = left_factor.shape[0]
    block_size = left_factor.shape[2]
    right_local = right_factor.shape[0]
    order_right = right_factor.shape[2]
    peer_count = lax.axis_size("blk")
    block_count = peer_count * local_blocks

    upstream = cotangent.reshape(row_count, right_local, order_right)
    right_full = swap_halves(right_factor, 1)
    eye = jnp.eye(row_count, dtype=jnp.bfloat16)
    upstream_t = jnp.einsum(
        "rc,rs->cs", cotangent, eye, preferred_element_type=jnp.float32
    ).astype(jnp.bfloat16)
    upstream_t = with_layout_constraint(upstream_t, Layout((0, 1)))
    upstream_t = upstream_t.reshape(right_local, order_right, row_count)
    back_grad = jnp.einsum(
        "jmr,jkm->kjr", upstream_t, right_full, preferred_element_type=jnp.float32
    ).astype(jnp.bfloat16)
    back_sent = back_grad.reshape(peer_count, local_blocks, right_local, row_count)
    back_got = lax.all_to_all(back_sent, "blk", 0, 0, tiled=True)

    unit_mask = (jnp.arange(block_size)[None, :] < session_units[:, None]).astype(jnp.bfloat16)
    inputs = units.reshape(row_count, local_blocks, block_size) * unit_mask[None]
    half_rows = block_size // 2
    core_here = lax.axis_index("bin")
    left_other = lax.ppermute(left_factor, "bin", [(0, 1), (1, 0)])
    own_inputs = lax.dynamic_slice_in_dim(inputs, core_here * half_rows, half_rows, axis=2)
    other_inputs = lax.dynamic_slice_in_dim(inputs, (1 - core_here) * half_rows, half_rows, axis=2)
    mixed = (
        jnp.einsum("rki,kij->jkr", own_inputs, left_factor, preferred_element_type=jnp.float32)
        + jnp.einsum("rki,kij->jkr", other_inputs, left_other, preferred_element_type=jnp.float32)
    ).astype(jnp.bfloat16)
    mixed_sent = mixed.reshape(peer_count, right_local, local_blocks, row_count)
    mixed_sent, back_got = lax.optimization_barrier((mixed_sent, back_got))

    half_size = block_size // 2
    core = lax.axis_index("bin")
    swap = [(0, 1), (1, 0)]
    own_part = lax.dynamic_slice_in_dim(inputs, core * half_size, half_size, axis=2)
    their_part = lax.dynamic_slice_in_dim(inputs, (1 - core) * half_size, half_size, axis=2)
    partner_part = lax.ppermute(their_part, "bin", swap)
    back_t = back_got.transpose(1, 0, 2, 3).reshape(local_blocks, block_size, row_count)
    partner_back = lax.ppermute(back_t, "bin", swap)
    mixed_sent = with_layout_constraint(mixed_sent, Layout((0, 1, 2, 3)))
    mixed_got = lax.all_to_all(mixed_sent, "blk", 0, 0, tiled=True)
    mixed_got = with_layout_constraint(mixed_got, Layout((0, 1, 2, 3)))
    left_term = jnp.einsum("rki,kjr->kij", own_part, back_t, preferred_element_type=jnp.float32)
    left_term = left_term + jnp.einsum(
        "rki,kjr->kij", partner_part, partner_back, preferred_element_type=jnp.float32
    )
    grad_left = left_term.astype(jnp.bfloat16)
    grad_left, mixed_got = lax.optimization_barrier((grad_left, mixed_got))
    half_peers = peer_count // 2

    def right_of(start, j_start, j_count):
        blocks = lax.dynamic_slice_in_dim(mixed_got, start, half_peers, axis=0)[:, j_start:j_start + j_count]
        blocks = blocks.transpose(1, 0, 2, 3).reshape(j_count, half_peers * local_blocks, row_count)
        rows = upstream[:, j_start:j_start + j_count]
        return jnp.einsum("jkr,rjm->jkm", blocks, rows, preferred_element_type=jnp.float32)

    half_j = right_local // 2
    sent_right = [right_of((1 - core) * half_peers, j0, half_j) for j0 in (0, half_j)]
    sent_right, mixed_got = lax.optimization_barrier((sent_right, mixed_got))
    got_right = jnp.concatenate(
        [lax.ppermute(part, "bin", [(0, 1), (1, 0)]) for part in sent_right], axis=0
    )
    own_right = lax.optimization_barrier(right_of(core * half_peers, 0, right_local))
    grad_right = (own_right + got_right).astype(jnp.bfloat16)
    return (grad_left, grad_right)


def solution(mesh):
    placed = (
        P(("grp", "bin"), "blk"),
        P(("grp", "bin"), "blk"),
        P("blk", "bin", None),
        P("blk", "bin", None),
        P(("grp", "blk")),
    )
    return jax.shard_map(
        on_device,
        mesh=mesh,
        in_specs=placed,
        out_specs=(P(("grp", "blk"), "bin", None), P(("grp", "blk"), "bin", None)),
        check_vma=False,
    )
```

```python
import jax
import jax.numpy as jnp
from jax import lax
from jax.sharding import PartitionSpec as P
from jax.experimental.layout import Layout, with_layout_constraint


def swap_halves(local, axis):
    other = lax.ppermute(local, "bin", [(0, 1), (1, 0)])
    core = lax.axis_index("bin")
    first = jnp.where(core == 0, local, other)
    second = jnp.where(core == 0, other, local)
    return jnp.concatenate([first, second], axis=axis)


def on_device(units, cotangent, left_factor, right_factor, session_units):
    row_count = units.shape[0]
    local_blocks = left_factor.shape[0]
    block_size = left_factor.shape[2]
    right_local = right_factor.shape[0]
    order_right = right_factor.shape[2]
    peer_count = lax.axis_size("blk")
    block_count = peer_count * local_blocks

    upstream = cotangent.reshape(row_count, right_local, order_right)
    right_full = swap_halves(right_factor, 1)
    eye = jnp.eye(row_count, dtype=jnp.bfloat16)
    upstream_t = jnp.einsum(
        "rc,rs->cs", cotangent, eye, preferred_element_type=jnp.float32
    ).astype(jnp.bfloat16)
    upstream_t = with_layout_constraint(upstream_t, Layout((0, 1)))
    upstream_t = upstream_t.reshape(right_local, order_right, row_count)
    back_grad = jnp.einsum(
        "jmr,jkm->kjr", upstream_t, right_full, preferred_element_type=jnp.float32
    ).astype(jnp.bfloat16)
    back_sent = back_grad.reshape(peer_count, local_blocks, right_local, row_count)
    back_got = lax.all_to_all(back_sent, "blk", 0, 0, tiled=True)

    unit_mask = (jnp.arange(block_size)[None, :] < session_units[:, None]).astype(jnp.bfloat16)
    inputs = units.reshape(row_count, local_blocks, block_size) * unit_mask[None]
    left_full = swap_halves(left_factor, 1)
    mixed = jnp.einsum(
        "rki,kij->jkr", inputs, left_full, preferred_element_type=jnp.float32
    ).astype(jnp.bfloat16)
    mixed_sent = mixed.reshape(peer_count, right_local, local_blocks, row_count)
    mixed_sent, back_got = lax.optimization_barrier((mixed_sent, back_got))

    half_size = block_size // 2
    core = lax.axis_index("bin")
    swap = [(0, 1), (1, 0)]
    own_part = lax.dynamic_slice_in_dim(inputs, core * half_size, half_size, axis=2)
    their_part = lax.dynamic_slice_in_dim(inputs, (1 - core) * half_size, half_size, axis=2)
    partner_part = lax.ppermute(their_part, "bin", swap)
    back_t = back_got.transpose(1, 0, 2, 3).reshape(local_blocks, block_size, row_count)
    partner_back = lax.ppermute(back_t, "bin", swap)
    mixed_sent = with_layout_constraint(mixed_sent, Layout((0, 1, 2, 3)))
    mixed_got = lax.all_to_all(mixed_sent, "blk", 0, 0, tiled=True)
    mixed_got = with_layout_constraint(mixed_got, Layout((0, 1, 2, 3)))
    left_term = jnp.einsum("rki,kjr->kij", own_part, back_t, preferred_element_type=jnp.float32)
    left_term = left_term + jnp.einsum(
        "rki,kjr->kij", partner_part, partner_back, preferred_element_type=jnp.float32
    )
    grad_left = left_term.astype(jnp.bfloat16)
    grad_left, mixed_got = lax.optimization_barrier((grad_left, mixed_got))
    half_peers = peer_count // 2

    def right_of(start, j_start, j_count):
        blocks = lax.dynamic_slice_in_dim(mixed_got, start, half_peers, axis=0)[:, j_start:j_start + j_count]
        blocks = blocks.transpose(1, 0, 2, 3).reshape(j_count, half_peers * local_blocks, row_count)
        rows = upstream[:, j_start:j_start + j_count]
        return jnp.einsum("jkr,rjm->jkm", blocks, rows, preferred_element_type=jnp.float32)

    half_j = right_local // 2
    theirs_all = right_of((1 - core) * half_peers, 0, right_local)
    sent_right = [theirs_all[:half_j], theirs_all[half_j:]]
    sent_right, mixed_got = lax.optimization_barrier((sent_right, mixed_got))
    got_right = jnp.concatenate(
        [lax.ppermute(part, "bin", [(0, 1), (1, 0)]) for part in sent_right], axis=0
    )
    own_right = lax.optimization_barrier(right_of(core * half_peers, 0, right_local))
    grad_right = (own_right + got_right).astype(jnp.bfloat16)
    return (grad_left, grad_right)


def solution(mesh):
    placed = (
        P(("grp", "bin"), "blk"),
        P(("grp", "bin"), "blk"),
        P("blk", "bin", None),
        P("blk", "bin", None),
        P(("grp", "blk")),
    )
    return jax.shard_map(
        on_device,
        mesh=mesh,
        in_specs=placed,
        out_specs=(P(("grp", "blk"), "bin", None), P(("grp", "blk"), "bin", None)),
        check_vma=False,
    )
```
